128 devices in a mesh: seq: 32 (over y, x, core), head: 4 (over z).
Axes of the slice: x: 4, y: 4, z: 4, core: 2. Of those that a mesh axis runs over, the one named last changes fastest.
Arguments:
- query_in: bfloat16 [8192, 4096], P('seq', 'head'), may hold values from -1200 to 1200
- key_in: bfloat16 [8192, 4096], P('seq', 'head'), may hold values from -1200 to 1200
- value_in: bfloat16 [8192, 4096], P('seq', 'head'), may hold values from -6 to 6
- out_grad: bfloat16 [8192, 4096], P('seq', 'head'), may hold values from -6 to 6
- query_gain: float32 [4096], P('head'), may hold values from 0.5 to 2
- key_gain: float32 [4096], P('head'), may hold values from 0.5 to 2
- random_blocks: int32 [128, 3], replicated, may hold values from 0 to 127, as said below
- global_blocks: int32 [2], replicated, may hold values from 0 to 127, as said below
Outputs:
- attn_out: bfloat16 [8192, 4096], P('seq', 'head')
- query_grad: bfloat16 [8192, 4096], P('seq', 'head')
- key_grad: bfloat16 [8192, 4096], P('seq', 'head')
- value_grad: bfloat16 [8192, 4096], P('seq', 'head')
The draws below stay inside these ranges and needn't reach their ends.
Inputs may be any that keep to these rules, and one draw needn't show every extreme that they name: `random_blocks`: for the 4 query blocks of one index of seq, at most 2 of their random entries name blocks of any one index of seq, and exactly 2 name blocks of some index of seq. `global_blocks`: the 2 global blocks are distinct, and one of them, at a position that varies, is the last block of the sequence.
All inputs are finite; a program needn't handle non-finite values.
Results may differ from the reference program's by a relative error of at most 0.04.
Values may be sent and summed in bfloat16 or wider, within the bound.
No kernel may reach another device: no remote copies, remote signals or barrier semaphores. Data moves between devices by JAX's collectives and lax.ppermute only.
A program may use at most 192 MiB of HBM per device.

```python
import math
import jax
import jax.numpy as jnp
from jax import lax

D = 4096
H = 32
HD = 128
BLK = 64
RAND = 3
GLOB = 2
TOKENS = 8192
NB = 128
QBD = 4
SHARDS = 32
CAP = 2


def query_key_pair(key):
    base = jax.random.fold_in(key, 17)
    first, second = jax.random.split(base, 2)
    query_vals = jnp.clip(jax.random.normal(first, (TOKENS, D), jnp.float32), -4.0, 4.0)
    key_vals = jnp.clip(jax.random.normal(second, (TOKENS, D), jnp.float32), -4.0, 4.0)
    columns = jnp.exp(jnp.log(3.0) * jnp.arange(D, dtype=jnp.float32) / D)
    query_vals = query_vals * columns[None, :]
    key_vals = key_vals * columns[None, :]
    return (query_vals, key_vals)


def draw_query_in(key, part):
    return query_key_pair(key)[0].astype(jnp.bfloat16)


def draw_key_in(key, part):
    return query_key_pair(key)[1].astype(jnp.bfloat16)


def draw_random_blocks(key, part):
    slot_count = RAND * QBD
    shard_keys = jax.random.split(jax.random.fold_in(key, 3), SHARDS)

    def one_shard(shard_key):
        key_hot, key_perm, key_place = jax.random.split(shard_key, 3)
        hottest = jax.random.randint(key_hot, (), 0, SHARDS)
        slot_ids = jnp.arange(slot_count)
        others = (hottest + 1 + (slot_ids - CAP) % (SHARDS - 1)) % SHARDS
        owners = jnp.where(slot_ids < CAP, hottest, others)
        owners = owners[jax.random.permutation(key_perm, slot_count)]
        places = jax.random.randint(key_place, (slot_count,), 0, QBD)
        return (owners * QBD + places).reshape(QBD, RAND)
    return jax.vmap(one_shard)(shard_keys).reshape(NB, RAND).astype(jnp.int32)


def draw_global_blocks(key, part):
    base = jax.random.fold_in(key, 5)
    key_pick, key_order = jax.random.split(base, 2)
    picked = jax.random.permutation(key_pick, NB - 1)[:GLOB - 1].astype(jnp.int32)
    chosen = jnp.concatenate([picked, jnp.full((1,), NB - 1, jnp.int32)])
    return chosen[jax.random.permutation(key_order, GLOB)].astype(jnp.int32)


def steps_of(rng, shape, pieces, smallest, high):
    level, own = 1.0, jax.random.fold_in(rng, 6)
    for position, blocks in pieces:
        heights = jnp.exp(jax.random.uniform(jax.random.fold_in(own, position), (blocks,), jnp.float32, smallest / len(pieces), high / len(pieces)))
        level = level * jnp.repeat(heights, shape[position] // blocks).reshape([-1 if axis == position else 1 for axis in range(len(shape))])
    return level


def normal_values(rng, extent, scale, most, shards=(), kind=jnp.bfloat16):
    array = scale * jax.random.normal(rng, extent, jnp.float32)
    if shards:
        array = array * steps_of(rng, extent, shards, -0.22, 0.18)
    return jnp.clip(array, -most, most).astype(kind)


def setup_inputs(seed: int = 0) -> dict:
    seeds = jax.random.split(jax.random.key(seed), 9)
    query_in = draw_query_in(jax.random.fold_in(seeds[8], 71), 0)
    key_in = draw_key_in(jax.random.fold_in(seeds[8], 71), 0)
    value_in = normal_values(seeds[2], (TOKENS, D), 1.0, 6.0, ((0, 32), (1, 4)))
    out_grad = normal_values(seeds[3], (TOKENS, D), 1.0, 6.0, ((0, 32), (1, 4)))
    query_gain = jnp.clip(jnp.exp(math.log(2.0) - 1.3862944 * jax.random.uniform(seeds[4], (D,), jnp.float32) ** steps_of(seeds[4], (D,), ((0, 4),), -0.2, 0.2)), 0.5, 2.0)
    key_gain = jnp.clip(jnp.exp(math.log(2.0) - 1.3862944 * jax.random.uniform(seeds[5], (D,), jnp.float32) ** steps_of(seeds[5], (D,), ((0, 4),), -0.2, 0.2)), 0.5, 2.0)
    random_blocks = draw_random_blocks(jax.random.fold_in(seeds[8], 71), 0)
    global_blocks = draw_global_blocks(jax.random.fold_in(seeds[8], 71), 0)
    return dict(query_in=query_in, key_in=key_in, value_in=value_in, out_grad=out_grad, query_gain=query_gain, key_gain=key_gain, random_blocks=random_blocks, global_blocks=global_blocks)


EPS = 1e-06
NEG = -1e+30

def normed(values, gain):
    full = values.astype(jnp.float32)
    inverse = lax.rsqrt(lax.optimization_barrier(jnp.sum(full * full, axis=1)) / D + EPS)
    return (full, inverse, (full * inverse[:, None] * gain[None, :]).astype(jnp.bfloat16))

def norm_grad(full, inverse, gain, grad):
    total = lax.optimization_barrier(jnp.sum(full * gain[None, :] * grad, axis=1))
    result = inverse[:, None] * gain[None, :] * grad - full * (inverse ** 3 * total / D)[:, None]
    return result.astype(jnp.bfloat16)

def round_trip(values):
    return lax.optimization_barrier(values.astype(jnp.bfloat16)).astype(jnp.float32)

def reference(query_in, key_in, value_in, out_grad, query_gain, key_gain, random_blocks, global_blocks):
    scale = HD ** (-0.5)
    list_len = 3 + RAND + GLOB
    block_total = TOKENS // BLK
    query_f, query_rms, query_normed = normed(query_in, query_gain)
    key_f, key_rms, key_normed = normed(key_in, key_gain)
    query_blk = query_normed.reshape(block_total, BLK, H, HD)
    key_blk = key_normed.reshape(block_total, BLK, H, HD)
    value_blk = value_in.reshape(block_total, BLK, H, HD)
    grad_blk = out_grad.reshape(block_total, BLK, H, HD)

    def block_step(carry, index):
        key_acc, value_acc = carry
        window_ids = jnp.stack([index - 1, index, index + 1]).astype(jnp.int32)
        list_ids = jnp.concatenate([window_ids, random_blocks[index].astype(jnp.int32), global_blocks.astype(jnp.int32)])
        valid = (list_ids >= 0) & (list_ids < block_total)
        clipped = jnp.clip(list_ids, 0, block_total - 1)
        keys_here = key_blk[clipped].reshape(list_len * BLK, H, HD).astype(jnp.float32)
        values_here = value_blk[clipped].reshape(list_len * BLK, H, HD).astype(jnp.float32)
        query_here = query_blk[index].astype(jnp.float32)
        grad_here = grad_blk[index].astype(jnp.float32)
        key_ok = jnp.repeat(valid, BLK)
        scores = jnp.einsum('qhd,khd->hqk', query_here, keys_here) * scale
        scores = jnp.where(key_ok[None, None, :], scores, NEG)
        top = lax.optimization_barrier(jnp.max(scores, axis=-1, keepdims=True))
        expd = jnp.exp(scores - top)
        prob = expd / lax.optimization_barrier(jnp.sum(expd, axis=-1, keepdims=True))
        prob_bf = round_trip(prob)
        out_block = jnp.einsum('hqk,khd->qhd', prob_bf, values_here).astype(jnp.bfloat16)
        delta = lax.optimization_barrier(jnp.sum(grad_here * out_block.astype(jnp.float32), axis=-1))
        dprob = jnp.einsum('qhd,khd->hqk', grad_here, values_here)
        dscore = prob * (dprob - jnp.transpose(delta)[:, :, None])
        dscore_bf = round_trip(dscore)
        dq_block = jnp.einsum('hqk,khd->qhd', dscore_bf, keys_here) * scale
        key_part = (jnp.einsum('hqk,qhd->khd', dscore_bf, query_here) * scale).reshape(list_len, BLK, H, HD)
        value_part = jnp.einsum('hqk,qhd->khd', prob_bf, grad_here).reshape(list_len, BLK, H, HD)
        key_part = jnp.concatenate([key_part[:3], round_trip(key_part[3:3 + RAND]), key_part[3 + RAND:]])
        value_part = jnp.concatenate([value_part[:3], round_trip(value_part[3:3 + RAND]), value_part[3 + RAND:]])
        key_acc = key_acc.at[clipped].add(key_part)
        value_acc = value_acc.at[clipped].add(value_part)
        return ((key_acc, value_acc), (out_block, dq_block))
    start = (jnp.zeros((block_total, BLK, H, HD), jnp.float32), jnp.zeros((block_total, BLK, H, HD), jnp.float32))
    (key_acc, value_acc), (out_blocks, dq_blocks) = lax.scan(block_step, start, jnp.arange(block_total, dtype=jnp.int32))
    attn_out = out_blocks.reshape(TOKENS, D)
    query_grad = norm_grad(query_f, query_rms, query_gain, dq_blocks.reshape(TOKENS, D))
    key_grad = norm_grad(key_f, key_rms, key_gain, key_acc.reshape(TOKENS, D))
    value_grad = value_acc.reshape(TOKENS, D).astype(jnp.bfloat16)
    return (attn_out, query_grad, key_grad, value_grad)
```

```python
import jax
import jax.numpy as jnp
from jax import lax
from jax.sharding import Mesh
from jax.sharding import PartitionSpec as P

D = 4096
HD = 128
BLK = 64
RAND = 3
GLOB = 2


EPS = 1e-06
NEG = -1e30


def ring_shifts(value, axis, count):
    pieces = [value]
    for d in range(1, count):
        perm = [(i, (i + d) % count) for i in range(count)]
        pieces.append(lax.ppermute(value, axis, perm))
    return pieces


def shards(
    query_in, key_in, value_in, out_grad, query_gain, key_gain, random_blocks, global_blocks
):
    tok_rows, feat_dim = query_in.shape
    heads = feat_dim // HD
    rows = lax.axis_size("y")
    my_row = lax.axis_index("y")
    row_tokens = tok_rows * heads
    row_blocks = row_tokens // BLK
    all_blocks = row_blocks * rows
    list_len = 3 + RAND + GLOB
    scale = HD ** (-0.5)

    query_f = query_in.astype(jnp.float32)
    key_f = key_in.astype(jnp.float32)
    sum_query, sum_key = lax.psum(
        (jnp.sum(query_f * query_f, axis=1), jnp.sum(key_f * key_f, axis=1)), "head"
    )
    query_rms = lax.rsqrt(sum_query / D + EPS)
    key_rms = lax.rsqrt(sum_key / D + EPS)
    query_normed = (query_f * query_rms[:, None] * query_gain[None, :]).astype(jnp.bfloat16)
    key_normed = (key_f * key_rms[:, None] * key_gain[None, :]).astype(jnp.bfloat16)

    stacked = jnp.stack([query_normed, key_normed, value_in, out_grad]).reshape(
        4, tok_rows, heads, HD
    )
    moved = lax.all_to_all(stacked, "xc", 2, 1, tiled=True).reshape(4, row_tokens, HD)
    query_h = moved[0].reshape(row_blocks, BLK, HD)
    grad_h = moved[3].reshape(row_blocks, BLK, HD)
    kv_own = moved[1:3].reshape(2, row_blocks, BLK, HD)

    kv_all = jnp.stack(ring_shifts(kv_own, "y", rows), axis=1).reshape(
        2, rows * row_blocks, BLK, HD
    )

    block_ids = my_row * row_blocks + jnp.arange(row_blocks, dtype=jnp.int32)
    my_random = lax.dynamic_slice_in_dim(random_blocks.astype(jnp.int32), my_row * row_blocks, row_blocks, 0)
    glob = global_blocks.astype(jnp.int32)
    list_ids = jnp.concatenate(
        [
            block_ids[:, None] - 1,
            block_ids[:, None],
            block_ids[:, None] + 1,
            my_random,
            jnp.broadcast_to(glob[None, :], (row_blocks, GLOB)),
        ],
        axis=1,
    )
    valid = (list_ids >= 0) & (list_ids < all_blocks)
    clipped = jnp.clip(list_ids, 0, all_blocks - 1)
    shift_pos = ((my_row - clipped // row_blocks) % rows) * row_blocks + clipped % row_blocks
    key_list = kv_all[0][shift_pos]
    value_list = kv_all[1][shift_pos]

    scores = (
        jnp.einsum("bqd,bekd->bqek", query_h, key_list, preferred_element_type=jnp.float32)
        * scale
    ).reshape(row_blocks, BLK, list_len * BLK)
    key_ok = jnp.repeat(valid, BLK, axis=1)
    scores = jnp.where(key_ok[:, None, :], scores, NEG)
    top = jnp.max(scores, axis=-1, keepdims=True)
    expd = jnp.exp(scores - top)
    totals = jnp.sum(expd, axis=-1, keepdims=True)
    prob = expd / totals
    prob_bf = prob.astype(jnp.bfloat16).reshape(row_blocks, BLK, list_len, BLK)
    out_h = jnp.einsum(
        "bqek,bekd->bqd", prob_bf, value_list, preferred_element_type=jnp.float32
    ).astype(jnp.bfloat16)
    delta = jnp.sum(grad_h.astype(jnp.float32) * out_h.astype(jnp.float32), axis=-1)
    dprob = jnp.einsum(
        "bqd,bekd->bqek", grad_h, value_list, preferred_element_type=jnp.float32
    ).reshape(row_blocks, BLK, list_len * BLK)
    dscore_bf = (prob * (dprob - delta[..., None])).astype(jnp.bfloat16).reshape(
        row_blocks, BLK, list_len, BLK
    )
    dq_h = (
        jnp.einsum("bqek,bekd->bqd", dscore_bf, key_list, preferred_element_type=jnp.float32)
        * scale
    )
    key_part = (
        jnp.einsum("bqek,bqd->bekd", dscore_bf, query_h, preferred_element_type=jnp.float32)
        * scale
    )
    value_part = jnp.einsum(
        "bqek,bqd->bekd", prob_bf, grad_h, preferred_element_type=jnp.float32
    )
    parts = jnp.stack([key_part, value_part])

    window = sum(
        jnp.pad(parts[:, :, offset], ((0, 0), (offset, 2 - offset), (0, 0), (0, 0)))
        for offset in range(3)
    )
    full = jnp.zeros((2, all_blocks + 2, BLK, HD), jnp.float32)
    full = lax.dynamic_update_slice(full, window, (0, my_row * row_blocks, 0, 0))
    full = full[:, 1 : all_blocks + 1]
    rand_parts = (
        parts[:, :, 3 : 3 + RAND].astype(jnp.bfloat16).reshape(2, row_blocks * RAND, BLK * HD)
    )
    onehot = (
        my_random.reshape(row_blocks * RAND)[None, :]
        == jnp.arange(all_blocks, dtype=jnp.int32)[:, None]
    ).astype(jnp.bfloat16)
    rand_sum = jnp.einsum(
        "nr,trx->tnx", onehot, rand_parts, preferred_element_type=jnp.float32
    ).reshape(2, all_blocks, BLK, HD)
    full = full + rand_sum
    glob_sum = jnp.sum(parts[:, :, 3 + RAND :], axis=1)
    full = full.at[:, glob].add(glob_sum)

    by_row = full.reshape(2, rows, row_blocks, BLK, HD)
    own = lax.dynamic_index_in_dim(by_row, my_row, 1, keepdims=False)
    for d in range(1, rows):
        target = (my_row + d) % rows
        piece = lax.dynamic_index_in_dim(by_row, target, 1, keepdims=False).astype(jnp.bfloat16)
        perm = [(i, (i + d) % rows) for i in range(rows)]
        own = own + lax.ppermute(piece, "y", perm).astype(jnp.float32)

    half = jnp.stack(
        [out_h.reshape(row_tokens, 1, HD), own[1].astype(jnp.bfloat16).reshape(row_tokens, 1, HD)]
    )
    wide = jnp.stack([dq_h.reshape(row_tokens, 1, HD), own[0].reshape(row_tokens, 1, HD)])
    half = lax.all_to_all(half, "xc", 1, 2, tiled=True).reshape(2, tok_rows, feat_dim)
    wide = lax.all_to_all(wide, "xc", 1, 2, tiled=True).reshape(2, tok_rows, feat_dim)
    attn_out = half[0]
    value_grad = half[1]
    dq_normed = wide[0]
    dk_normed = wide[1]

    dot_query = jnp.sum(query_f * query_gain[None, :] * dq_normed, axis=1)
    dot_key = jnp.sum(key_f * key_gain[None, :] * dk_normed, axis=1)
    total_query, total_key = lax.psum((dot_query, dot_key), "head")
    query_grad = (
        query_rms[:, None] * query_gain[None, :] * dq_normed
        - query_f * (query_rms**3 * total_query / D)[:, None]
    ).astype(jnp.bfloat16)
    key_grad = (
        key_rms[:, None] * key_gain[None, :] * dk_normed
        - key_f * (key_rms**3 * total_key / D)[:, None]
    ).astype(jnp.bfloat16)
    return (attn_out, query_grad, key_grad, value_grad)


def solution(mesh):
    seq = mesh.shape["seq"]
    head = mesh.shape["head"]
    row = D // head // HD
    sub = Mesh(mesh.devices.reshape(seq // row, row, head), ("y", "xc", "head"))
    tok = P(("y", "xc"), "head")
    in_specs = (tok, tok, tok, tok, P("head"), P("head"), P(), P())
    out_specs = (tok, tok, tok, tok)
    return jax.shard_map(shards, mesh=sub, in_specs=in_specs, out_specs=out_specs, check_vma=False)
```

```python
import jax
import jax.numpy as jnp
from jax import lax
from jax.sharding import Mesh
from jax.sharding import PartitionSpec as P

D = 4096
HD = 128
BLK = 64
RAND = 3
GLOB = 2


EPS = 1e-06
NEG = -1e30


def ring_shifts(value, axis, count):
    pieces = [value]
    for d in range(1, count):
        perm = [(i, (i + d) % count) for i in range(count)]
        pieces.append(lax.ppermute(value, axis, perm))
    return pieces


def shards(
    query_in, key_in, value_in, out_grad, query_gain, key_gain, random_blocks, global_blocks
):
    tok_rows, feat_dim = query_in.shape
    heads = feat_dim // HD
    rows = lax.axis_size("y")
    my_row = lax.axis_index("y")
    row_tokens = tok_rows * heads
    row_blocks = row_tokens // BLK
    all_blocks = row_blocks * rows
    list_len = 3 + RAND + GLOB
    scale = HD ** (-0.5)

    query_f = query_in.astype(jnp.float32)
    key_f = key_in.astype(jnp.float32)
    sum_query, sum_key = lax.psum(
        (jnp.sum(query_f * query_f, axis=1), jnp.sum(key_f * key_f, axis=1)), "head"
    )
    query_rms = lax.rsqrt(sum_query / D + EPS)
    key_rms = lax.rsqrt(sum_key / D + EPS)
    query_normed = (query_f * query_rms[:, None] * query_gain[None, :]).astype(jnp.bfloat16)
    key_normed = (key_f * key_rms[:, None] * key_gain[None, :]).astype(jnp.bfloat16)

    def to_head(arrays):
        stacked = jnp.stack(arrays).reshape(len(arrays), tok_rows, heads, HD)
        moved = lax.all_to_all(stacked, "xc", 2, 1, tiled=True)
        return moved.reshape(len(arrays), row_blocks, BLK, HD)

    kv_own = to_head([key_normed, value_in])
    qg = to_head([query_normed, out_grad])
    query_h = qg[0]
    grad_h = qg[1]

    kv_all = jnp.stack(ring_shifts(kv_own, "y", rows), axis=1).reshape(
        2, rows * row_blocks, BLK, HD
    )

    block_ids = my_row * row_blocks + jnp.arange(row_blocks, dtype=jnp.int32)
    my_random = lax.dynamic_slice_in_dim(random_blocks.astype(jnp.int32), my_row * row_blocks, row_blocks, 0)
    glob = global_blocks.astype(jnp.int32)
    list_ids = jnp.concatenate(
        [
            block_ids[:, None] - 1,
            block_ids[:, None],
            block_ids[:, None] + 1,
            my_random,
            jnp.broadcast_to(glob[None, :], (row_blocks, GLOB)),
        ],
        axis=1,
    )
    valid = (list_ids >= 0) & (list_ids < all_blocks)
    clipped = jnp.clip(list_ids, 0, all_blocks - 1)
    shift_pos = ((my_row - clipped // row_blocks) % rows) * row_blocks + clipped % row_blocks
    key_list = kv_all[0][shift_pos]
    value_list = kv_all[1][shift_pos]

    scores = (
        jnp.einsum("bqd,bekd->bqek", query_h, key_list, preferred_element_type=jnp.float32)
        * scale
    ).reshape(row_blocks, BLK, list_len * BLK)
    key_ok = jnp.repeat(valid, BLK, axis=1)
    scores = jnp.where(key_ok[:, None, :], scores, NEG)
    top = jnp.max(scores, axis=-1, keepdims=True)
    expd = jnp.exp(scores - top)
    totals = jnp.sum(expd, axis=-1, keepdims=True)
    prob = expd / totals
    prob_bf = prob.astype(jnp.bfloat16).reshape(row_blocks, BLK, list_len, BLK)
    out_h = jnp.einsum(
        "bqek,bekd->bqd", prob_bf, value_list, preferred_element_type=jnp.float32
    ).astype(jnp.bfloat16)
    delta = jnp.sum(grad_h.astype(jnp.float32) * out_h.astype(jnp.float32), axis=-1)
    dprob = jnp.einsum(
        "bqd,bekd->bqek", grad_h, value_list, preferred_element_type=jnp.float32
    ).reshape(row_blocks, BLK, list_len * BLK)
    dscore_bf = (prob * (dprob - delta[..., None])).astype(jnp.bfloat16).reshape(
        row_blocks, BLK, list_len, BLK
    )
    dq_h = (
        jnp.einsum("bqek,bekd->bqd", dscore_bf, key_list, preferred_element_type=jnp.float32)
        * scale
    )
    key_part = (
        jnp.einsum("bqek,bqd->bekd", dscore_bf, query_h, preferred_element_type=jnp.float32)
        * scale
    )
    value_part = jnp.einsum(
        "bqek,bqd->bekd", prob_bf, grad_h, preferred_element_type=jnp.float32
    )
    parts = jnp.stack([key_part, value_part])
    is_rand = (jnp.arange(list_len) >= 3) & (jnp.arange(list_len) < 3 + RAND)
    parts = jnp.where(
        is_rand[None, None, :, None, None],
        lax.reduce_precision(parts, exponent_bits=8, mantissa_bits=7),
        parts,
    ).reshape(2, row_blocks * list_len, BLK * HD)

    target = ((list_ids // row_blocks - my_row) % rows) * row_blocks + list_ids % row_blocks
    target = jnp.where(valid, target, -1).reshape(row_blocks * list_len)
    onehot = (
        target[None, :] == jnp.arange(all_blocks, dtype=jnp.int32)[:, None]
    ).astype(jnp.float32)
    placed = jnp.einsum(
        "ts,asx->atx", onehot, parts, precision=lax.Precision.HIGHEST,
        preferred_element_type=jnp.float32,
    ).reshape(2, rows, row_blocks, BLK, HD)

    own = placed[:, 0]
    for d in range(1, rows):
        perm = [(i, (i + d) % rows) for i in range(rows)]
        own = own + lax.ppermute(placed[:, d].astype(jnp.bfloat16), "y", perm).astype(jnp.float32)

    def to_tokens(arrays):
        stacked = jnp.stack([a.reshape(row_tokens, 1, HD) for a in arrays])
        moved = lax.all_to_all(stacked, "xc", 1, 2, tiled=True)
        return moved.reshape(len(arrays), tok_rows, feat_dim)

    early = to_tokens([out_h.astype(jnp.float32), dq_h])
    attn_out = early[0].astype(jnp.bfloat16)
    dq_normed = early[1]
    late = to_tokens([own[0].astype(jnp.bfloat16), own[1].astype(jnp.bfloat16)])
    dk_normed = late[0].astype(jnp.float32)
    value_grad = late[1]

    total_query = lax.psum(jnp.sum(query_f * query_gain[None, :] * dq_normed, axis=1), "head")
    total_key = lax.psum(jnp.sum(key_f * key_gain[None, :] * dk_normed, axis=1), "head")
    query_grad = (
        query_rms[:, None] * query_gain[None, :] * dq_normed
        - query_f * (query_rms**3 * total_query / D)[:, None]
    ).astype(jnp.bfloat16)
    key_grad = (
        key_rms[:, None] * key_gain[None, :] * dk_normed
        - key_f * (key_rms**3 * total_key / D)[:, None]
    ).astype(jnp.bfloat16)
    return (attn_out, query_grad, key_grad, value_grad)


def solution(mesh):
    seq = mesh.shape["seq"]
    head = mesh.shape["head"]
    row = D // head // HD
    sub = Mesh(mesh.devices.reshape(seq // row, row, head), ("y", "xc", "head"))
    tok = P(("y", "xc"), "head")
    in_specs = (tok, tok, tok, tok, P("head"), P("head"), P(), P())
    out_specs = (tok, tok, tok, tok)
    return jax.shard_map(shards, mesh=sub, in_specs=in_specs, out_specs=out_specs, check_vma=False)
```

```python
import jax
import jax.numpy as jnp
import functools

from jax import lax
from jax.experimental import pallas as pl
from jax.experimental.pallas import tpu as pltpu
from jax.sharding import Mesh
from jax.sharding import PartitionSpec as P

D = 4096
HD = 128
BLK = 64
RAND = 3
GLOB = 2


EPS = 1e-06
NEG = -1e30


def attn_kernel(src_ref, tgt_ref, ok_ref, q_ref, g_ref, k_ref, v_ref,
                o_ref, dq_ref, dk_ref, dv_ref, *, entries, rand_lo, rand_hi, scale):
    b = pl.program_id(0)

    @pl.when(b == 0)
    def _():
        dk_ref[...] = jnp.zeros_like(dk_ref)
        dv_ref[...] = jnp.zeros_like(dv_ref)

    q = q_ref[0]
    g = g_ref[0]
    keys = jnp.concatenate([k_ref[src_ref[b, e]] for e in range(entries)], axis=0)
    vals = jnp.concatenate([v_ref[src_ref[b, e]] for e in range(entries)], axis=0)
    lane_entry = lax.broadcasted_iota(jnp.int32, (1, entries * BLK), 1) // BLK
    ok = jnp.zeros((1, entries * BLK), jnp.int32)
    for e in range(entries):
        ok = jnp.where(lane_entry == e, ok_ref[b, e], ok)
    scores = lax.dot_general(q, keys, (((1,), (1,)), ((), ())),
                             preferred_element_type=jnp.float32) * scale
    scores = jnp.where(ok > 0, scores, NEG)
    top = jnp.max(scores, axis=1, keepdims=True)
    expd = jnp.exp(scores - top)
    prob = expd / jnp.sum(expd, axis=1, keepdims=True)
    prob_bf = prob.astype(jnp.bfloat16)
    out = jnp.dot(prob_bf, vals, preferred_element_type=jnp.float32).astype(jnp.bfloat16)
    o_ref[0] = out
    delta = jnp.sum(g.astype(jnp.float32) * out.astype(jnp.float32), axis=1, keepdims=True)
    dprob = lax.dot_general(g, vals, (((1,), (1,)), ((), ())),
                            preferred_element_type=jnp.float32)
    dscore_bf = (prob * (dprob - delta)).astype(jnp.bfloat16)
    dq_ref[0] = jnp.dot(dscore_bf, keys, preferred_element_type=jnp.float32) * scale
    dk_parts = lax.dot_general(dscore_bf, q, (((0,), (0,)), ((), ())),
                               preferred_element_type=jnp.float32) * scale
    dv_parts = lax.dot_general(prob_bf, g, (((0,), (0,)), ((), ())),
                               preferred_element_type=jnp.float32)
    for e in range(entries):
        pk = dk_parts[e * BLK:(e + 1) * BLK]
        pv = dv_parts[e * BLK:(e + 1) * BLK]
        if rand_lo <= e < rand_hi:
            pk = pk.astype(jnp.bfloat16).astype(jnp.float32)
            pv = pv.astype(jnp.bfloat16).astype(jnp.float32)
        t = tgt_ref[b, e]
        dk_ref[t] = dk_ref[t] + pk
        dv_ref[t] = dv_ref[t] + pv


def attention(src, tgt, ok, q, g, k_all, v_all, *, rand_lo, rand_hi, scale):
    nq, entries = src.shape
    nk = k_all.shape[0]
    kern = functools.partial(attn_kernel, entries=entries, rand_lo=rand_lo, rand_hi=rand_hi, scale=scale)
    blk = lambda b, *_: (b, 0, 0)
    whole = lambda b, *_: (0, 0, 0)
    grid_spec = pltpu.PrefetchScalarGridSpec(
        num_scalar_prefetch=3,
        grid=(nq,),
        in_specs=[
            pl.BlockSpec((1, BLK, HD), blk),
            pl.BlockSpec((1, BLK, HD), blk),
            pl.BlockSpec((nk, BLK, HD), whole),
            pl.BlockSpec((nk, BLK, HD), whole),
        ],
        out_specs=[
            pl.BlockSpec((1, BLK, HD), blk),
            pl.BlockSpec((1, BLK, HD), blk),
            pl.BlockSpec((nk, BLK, HD), whole),
            pl.BlockSpec((nk, BLK, HD), whole),
        ],
    )
    return pl.pallas_call(
        kern,
        grid_spec=grid_spec,
        out_shape=[
            jax.ShapeDtypeStruct((nq, BLK, HD), jnp.bfloat16),
            jax.ShapeDtypeStruct((nq, BLK, HD), jnp.float32),
            jax.ShapeDtypeStruct((nk, BLK, HD), jnp.float32),
            jax.ShapeDtypeStruct((nk, BLK, HD), jnp.float32),
        ],
        compiler_params=pltpu.CompilerParams(dimension_semantics=("arbitrary",), vmem_limit_bytes=48 * 1024 * 1024),
    )(src, tgt, ok, q, g, k_all, v_all)


def ring_shifts(value, axis, count):
    pieces = [value]
    for d in range(1, count):
        perm = [(i, (i + d) % count) for i in range(count)]
        pieces.append(lax.ppermute(value, axis, perm))
    return pieces


def shards(
    query_in, key_in, value_in, out_grad, query_gain, key_gain, random_blocks, global_blocks
):
    tok_rows, feat_dim = query_in.shape
    heads = feat_dim // HD
    rows = lax.axis_size("y")
    my_row = lax.axis_index("y")
    row_tokens = tok_rows * heads
    row_blocks = row_tokens // BLK
    all_blocks = row_blocks * rows
    list_len = 3 + RAND + GLOB
    scale = HD ** (-0.5)

    query_f = query_in.astype(jnp.float32)
    key_f = key_in.astype(jnp.float32)
    sum_query, sum_key = lax.psum(
        (jnp.sum(query_f * query_f, axis=1), jnp.sum(key_f * key_f, axis=1)), "head"
    )
    query_rms = lax.rsqrt(sum_query / D + EPS)
    key_rms = lax.rsqrt(sum_key / D + EPS)
    query_normed = (query_f * query_rms[:, None] * query_gain[None, :]).astype(jnp.bfloat16)
    key_normed = (key_f * key_rms[:, None] * key_gain[None, :]).astype(jnp.bfloat16)

    def to_head(arrays):
        stacked = jnp.stack(arrays).reshape(len(arrays), tok_rows, heads, HD)
        moved = lax.all_to_all(stacked, "xc", 2, 1, tiled=True)
        return moved.reshape(len(arrays), row_blocks, BLK, HD)

    kv_own = to_head([key_normed, value_in])
    qg = to_head([query_normed, out_grad])
    query_h = qg[0]
    grad_h = qg[1]

    kv_all = jnp.stack(ring_shifts(kv_own, "y", rows), axis=1).reshape(
        2, rows * row_blocks, BLK, HD
    )

    block_ids = my_row * row_blocks + jnp.arange(row_blocks, dtype=jnp.int32)
    my_random = lax.dynamic_slice_in_dim(random_blocks.astype(jnp.int32), my_row * row_blocks, row_blocks, 0)
    glob = global_blocks.astype(jnp.int32)
    list_ids = jnp.concatenate(
        [
            block_ids[:, None] - 1,
            block_ids[:, None],
            block_ids[:, None] + 1,
            my_random,
            jnp.broadcast_to(glob[None, :], (row_blocks, GLOB)),
        ],
        axis=1,
    )
    valid = (list_ids >= 0) & (list_ids < all_blocks)
    clipped = jnp.clip(list_ids, 0, all_blocks - 1)
    shift_pos = ((my_row - clipped // row_blocks) % rows) * row_blocks + clipped % row_blocks
    target = ((clipped // row_blocks - my_row) % rows) * row_blocks + clipped % row_blocks
    out_h, dq_h, dk_t, dv_t = attention(
        shift_pos, target, valid.astype(jnp.int32), query_h, grad_h, kv_all[0], kv_all[1],
        rand_lo=3, rand_hi=3 + RAND, scale=scale,
    )

    own_k = dk_t[:row_blocks]
    own_v = dv_t[:row_blocks]
    for d in range(1, rows):
        perm = [(i, (i + d) % rows) for i in range(rows)]
        piece = lax.slice_in_dim(dk_t, d * row_blocks, (d + 1) * row_blocks, axis=0)
        own_k = own_k + lax.ppermute(piece.astype(jnp.bfloat16), "y", perm).astype(jnp.float32)
        piece = lax.slice_in_dim(dv_t, d * row_blocks, (d + 1) * row_blocks, axis=0)
        own_v = own_v + lax.ppermute(piece.astype(jnp.bfloat16), "y", perm).astype(jnp.float32)

    def to_tokens(arrays):
        stacked = jnp.stack([a.reshape(row_tokens, 1, HD) for a in arrays])
        moved = lax.all_to_all(stacked, "xc", 1, 2, tiled=True)
        return moved.reshape(len(arrays), tok_rows, feat_dim)

    early = to_tokens([out_h.astype(jnp.float32), dq_h])
    attn_out = early[0].astype(jnp.bfloat16)
    dq_normed = early[1]
    late = to_tokens([own_k.astype(jnp.bfloat16), own_v.astype(jnp.bfloat16)])
    dk_normed = late[0].astype(jnp.float32)
    value_grad = late[1]

    total_query = lax.psum(jnp.sum(query_f * query_gain[None, :] * dq_normed, axis=1), "head")
    total_key = lax.psum(jnp.sum(key_f * key_gain[None, :] * dk_normed, axis=1), "head")
    query_grad = (
        query_rms[:, None] * query_gain[None, :] * dq_normed
        - query_f * (query_rms**3 * total_query / D)[:, None]
    ).astype(jnp.bfloat16)
    key_grad = (
        key_rms[:, None] * key_gain[None, :] * dk_normed
        - key_f * (key_rms**3 * total_key / D)[:, None]
    ).astype(jnp.bfloat16)
    return (attn_out, query_grad, key_grad, value_grad)


def solution(mesh):
    seq = mesh.shape["seq"]
    head = mesh.shape["head"]
    row = D // head // HD
    sub = Mesh(mesh.devices.reshape(seq // row, row, head), ("y", "xc", "head"))
    tok = P(("y", "xc"), "head")
    in_specs = (tok, tok, tok, tok, P("head"), P("head"), P(), P())
    out_specs = (tok, tok, tok, tok)
    return jax.shard_map(shards, mesh=sub, in_specs=in_specs, out_specs=out_specs, check_vma=False)
```

```python
import jax
import jax.numpy as jnp
import functools

from jax import lax
from jax.experimental import pallas as pl
from jax.experimental.pallas import tpu as pltpu
from jax.sharding import Mesh
from jax.sharding import PartitionSpec as P

D = 4096
HD = 128
BLK = 64
RAND = 3
GLOB = 2


EPS = 1e-06
NEG = -1e30


def attn_kernel(src_ref, tgt_ref, ok_ref, q_ref, g_ref, k_ref, v_ref,
                o_ref, dq_ref, dk_ref, dv_ref, *, entries, rand_lo, rand_hi, scale):
    b = pl.program_id(0)

    @pl.when(b == 0)
    def _():
        dk_ref[...] = jnp.zeros_like(dk_ref)
        dv_ref[...] = jnp.zeros_like(dv_ref)

    q = q_ref[0]
    g = g_ref[0]
    keys = jnp.concatenate([k_ref[src_ref[b, e]] for e in range(entries)], axis=0)
    vals = jnp.concatenate([v_ref[src_ref[b, e]] for e in range(entries)], axis=0)
    lane_entry = lax.broadcasted_iota(jnp.int32, (1, entries * BLK), 1) // BLK
    ok = jnp.zeros((1, entries * BLK), jnp.int32)
    for e in range(entries):
        ok = jnp.where(lane_entry == e, ok_ref[b, e], ok)
    scores = lax.dot_general(q, keys, (((1,), (1,)), ((), ())),
                             preferred_element_type=jnp.float32) * scale
    scores = jnp.where(ok > 0, scores, NEG)
    top = jnp.max(scores, axis=1, keepdims=True)
    expd = jnp.exp(scores - top)
    prob = expd / jnp.sum(expd, axis=1, keepdims=True)
    prob_bf = prob.astype(jnp.bfloat16)
    out = jnp.dot(prob_bf, vals, preferred_element_type=jnp.float32).astype(jnp.bfloat16)
    o_ref[0] = out
    delta = jnp.sum(g.astype(jnp.float32) * out.astype(jnp.float32), axis=1, keepdims=True)
    dprob = lax.dot_general(g, vals, (((1,), (1,)), ((), ())),
                            preferred_element_type=jnp.float32)
    dscore_bf = (prob * (dprob - delta)).astype(jnp.bfloat16)
    dq_ref[0] = jnp.dot(dscore_bf, keys, preferred_element_type=jnp.float32) * scale
    dk_parts = lax.dot_general(dscore_bf, q, (((0,), (0,)), ((), ())),
                               preferred_element_type=jnp.float32) * scale
    dv_parts = lax.dot_general(prob_bf, g, (((0,), (0,)), ((), ())),
                               preferred_element_type=jnp.float32)
    for e in range(entries):
        pk = dk_parts[e * BLK:(e + 1) * BLK]
        pv = dv_parts[e * BLK:(e + 1) * BLK]
        if rand_lo <= e < rand_hi:
            pk = pk.astype(jnp.bfloat16).astype(jnp.float32)
            pv = pv.astype(jnp.bfloat16).astype(jnp.float32)
        t = tgt_ref[b, e]
        dk_ref[t] = dk_ref[t] + pk
        dv_ref[t] = dv_ref[t] + pv


def attention(src, tgt, ok, q, g, k_all, v_all, *, rand_lo, rand_hi, scale):
    nq, entries = src.shape
    nk = k_all.shape[0]
    kern = functools.partial(attn_kernel, entries=entries, rand_lo=rand_lo, rand_hi=rand_hi, scale=scale)
    blk = lambda b, *_: (b, 0, 0)
    whole = lambda b, *_: (0, 0, 0)
    grid_spec = pltpu.PrefetchScalarGridSpec(
        num_scalar_prefetch=3,
        grid=(nq,),
        in_specs=[
            pl.BlockSpec((1, BLK, HD), blk),
            pl.BlockSpec((1, BLK, HD), blk),
            pl.BlockSpec((nk, BLK, HD), whole),
            pl.BlockSpec((nk, BLK, HD), whole),
        ],
        out_specs=[
            pl.BlockSpec((1, BLK, HD), blk),
            pl.BlockSpec((1, BLK, HD), blk),
            pl.BlockSpec((nk, BLK, HD), whole),
            pl.BlockSpec((nk, BLK, HD), whole),
        ],
    )
    return pl.pallas_call(
        kern,
        grid_spec=grid_spec,
        out_shape=[
            jax.ShapeDtypeStruct((nq, BLK, HD), jnp.bfloat16),
            jax.ShapeDtypeStruct((nq, BLK, HD), jnp.float32),
            jax.ShapeDtypeStruct((nk, BLK, HD), jnp.float32),
            jax.ShapeDtypeStruct((nk, BLK, HD), jnp.float32),
        ],
        compiler_params=pltpu.CompilerParams(dimension_semantics=("arbitrary",), vmem_limit_bytes=48 * 1024 * 1024),
    )(src, tgt, ok, q, g, k_all, v_all)


def ring_gather(value, axis, count):
    fwd = [(i, (i + 1) % count) for i in range(count)]
    bwd = [(i, (i - 1) % count) for i in range(count)]
    prev = lax.ppermute(value, axis, fwd)
    nxt = lax.ppermute(value, axis, bwd)
    half = value.shape[0] // 2
    far = jnp.concatenate(
        [
            lax.ppermute(prev[:half], axis, fwd),
            lax.ppermute(nxt[half:], axis, bwd),
        ]
    )
    return [value, prev, far, nxt]


def ring_reduce(pieces, axis, count):
    fwd = [(i, (i + 1) % count) for i in range(count)]
    bwd = [(i, (i - 1) % count) for i in range(count)]
    own, nxt, far, prev = pieces
    half = own.shape[0] // 2
    bf = lambda x: x.astype(jnp.bfloat16)
    f32 = lambda x: x.astype(jnp.float32)
    got_f = lax.ppermute((bf(nxt[half:]), bf(far[:half])), axis, fwd)
    got_b = lax.ppermute((bf(prev[:half]), bf(far[half:])), axis, bwd)
    late_f = lax.ppermute(bf(nxt[:half] + f32(got_f[1])), axis, fwd)
    late_b = lax.ppermute(bf(prev[half:] + f32(got_b[1])), axis, bwd)
    low = own[:half] + f32(got_b[0]) + f32(late_f)
    high = own[half:] + f32(got_f[0]) + f32(late_b)
    return jnp.concatenate([low, high])


def shards(
    query_in, key_in, value_in, out_grad, query_gain, key_gain, random_blocks, global_blocks
):
    tok_rows, feat_dim = query_in.shape
    heads = feat_dim // HD
    rows = lax.axis_size("y")
    my_row = lax.axis_index("y")
    row_tokens = tok_rows * heads
    row_blocks = row_tokens // BLK
    all_blocks = row_blocks * rows
    list_len = 3 + RAND + GLOB
    scale = HD ** (-0.5)

    def to_head(arrays):
        stacked = jnp.stack(arrays).reshape(len(arrays), tok_rows, heads, HD)
        stacked = stacked.transpose(0, 2, 1, 3)
        moved = lax.all_to_all(stacked, "xc", 1, 1, tiled=True)
        return moved.reshape(len(arrays), row_blocks, BLK, HD)

    vg = to_head([value_in, out_grad])

    query_f = query_in.astype(jnp.float32)
    key_f = key_in.astype(jnp.float32)
    sum_query, sum_key = lax.psum(
        (jnp.sum(query_f * query_f, axis=1), jnp.sum(key_f * key_f, axis=1)), "head"
    )
    query_rms = lax.rsqrt(sum_query / D + EPS)
    key_rms = lax.rsqrt(sum_key / D + EPS)
    query_normed = (query_f * query_rms[:, None] * query_gain[None, :]).astype(jnp.bfloat16)
    key_normed = (key_f * key_rms[:, None] * key_gain[None, :]).astype(jnp.bfloat16)

    kq = to_head([key_normed, query_normed])
    query_h = kq[1]
    grad_h = vg[1]

    k_all = jnp.concatenate(ring_gather(kq[0], "y", rows))
    v_all = jnp.concatenate(ring_gather(vg[0], "y", rows))

    block_ids = my_row * row_blocks + jnp.arange(row_blocks, dtype=jnp.int32)
    my_random = lax.dynamic_slice_in_dim(random_blocks.astype(jnp.int32), my_row * row_blocks, row_blocks, 0)
    glob = global_blocks.astype(jnp.int32)
    list_ids = jnp.concatenate(
        [
            block_ids[:, None] - 1,
            block_ids[:, None],
            block_ids[:, None] + 1,
            my_random,
            jnp.broadcast_to(glob[None, :], (row_blocks, GLOB)),
        ],
        axis=1,
    )
    valid = (list_ids >= 0) & (list_ids < all_blocks)
    clipped = jnp.clip(list_ids, 0, all_blocks - 1)
    shift_pos = ((my_row - clipped // row_blocks) % rows) * row_blocks + clipped % row_blocks
    target = ((clipped // row_blocks - my_row) % rows) * row_blocks + clipped % row_blocks
    out_h, dq_h, dk_t, dv_t = attention(
        shift_pos, target, valid.astype(jnp.int32), query_h, grad_h, k_all, v_all,
        rand_lo=3, rand_hi=3 + RAND, scale=scale,
    )

    split = lambda x: [x[d * row_blocks : (d + 1) * row_blocks] for d in range(rows)]
    own_k = ring_reduce(split(dk_t), "y", rows)
    own_v = ring_reduce(split(dv_t), "y", rows)

    def to_tokens(arrays):
        stacked = jnp.stack([a.reshape(heads, tok_rows, HD) for a in arrays])
        moved = lax.all_to_all(stacked, "xc", 1, 1, tiled=True)
        return moved.transpose(0, 2, 1, 3).reshape(len(arrays), tok_rows, feat_dim)

    early = to_tokens([out_h.astype(jnp.float32), dq_h])
    attn_out = early[0].astype(jnp.bfloat16)
    dq_normed = early[1]
    late = to_tokens([own_k.astype(jnp.bfloat16), own_v.astype(jnp.bfloat16)])
    dk_normed = late[0].astype(jnp.float32)
    value_grad = late[1]

    total_query = lax.psum(jnp.sum(query_f * query_gain[None, :] * dq_normed, axis=1), "head")
    total_key = lax.psum(jnp.sum(key_f * key_gain[None, :] * dk_normed, axis=1), "head")
    query_grad = (
        query_rms[:, None] * query_gain[None, :] * dq_normed
        - query_f * (query_rms**3 * total_query / D)[:, None]
    ).astype(jnp.bfloat16)
    key_grad = (
        key_rms[:, None] * key_gain[None, :] * dk_normed
        - key_f * (key_rms**3 * total_key / D)[:, None]
    ).astype(jnp.bfloat16)
    return (attn_out, query_grad, key_grad, value_grad)


def solution(mesh):
    seq = mesh.shape["seq"]
    head = mesh.shape["head"]
    row = D // head // HD
    sub = Mesh(mesh.devices.reshape(seq // row, row, head), ("y", "xc", "head"))
    tok = P(("y", "xc"), "head")
    in_specs = (tok, tok, tok, tok, P("head"), P("head"), P(), P())
    out_specs = (tok, tok, tok, tok)
    return jax.shard_map(shards, mesh=sub, in_specs=in_specs, out_specs=out_specs, check_vma=False)
```

```python
import jax
import jax.numpy as jnp
import functools

from jax import lax
from jax.experimental import pallas as pl
from jax.experimental.pallas import tpu as pltpu
from jax.sharding import Mesh

from jax.sharding import PartitionSpec as P

D = 4096
HD = 128
BLK = 64
RAND = 3
GLOB = 2


EPS = 1e-06
NEG = -1e30


def attn_kernel(src_ref, tgt_ref, ok_ref, q_ref, g_ref, k_ref, v_ref,
                o_ref, dq_ref, dk_ref, dv_ref, *, entries, rand_lo, rand_hi, scale):
    b = pl.program_id(0)

    @pl.when(b == 0)
    def _():
        dk_ref[...] = jnp.zeros_like(dk_ref)
        dv_ref[...] = jnp.zeros_like(dv_ref)

    q = q_ref[0]
    g = g_ref[0]
    keys = jnp.concatenate([k_ref[src_ref[b, e]] for e in range(entries)], axis=0)
    vals = jnp.concatenate([v_ref[src_ref[b, e]] for e in range(entries)], axis=0)
    lane_entry = lax.broadcasted_iota(jnp.int32, (1, entries * BLK), 1) // BLK
    ok = jnp.zeros((1, entries * BLK), jnp.int32)
    for e in range(entries):
        ok = jnp.where(lane_entry == e, ok_ref[b, e], ok)
    scores = lax.dot_general(q, keys, (((1,), (1,)), ((), ())),
                             preferred_element_type=jnp.float32) * scale
    scores = jnp.where(ok > 0, scores, NEG)
    top = jnp.max(scores, axis=1, keepdims=True)
    expd = jnp.exp(scores - top)
    prob = expd / jnp.sum(expd, axis=1, keepdims=True)
    prob_bf = prob.astype(jnp.bfloat16)
    out = jnp.dot(prob_bf, vals, preferred_element_type=jnp.float32).astype(jnp.bfloat16)
    o_ref[0] = out
    delta = jnp.sum(g.astype(jnp.float32) * out.astype(jnp.float32), axis=1, keepdims=True)
    dprob = lax.dot_general(g, vals, (((1,), (1,)), ((), ())),
                            preferred_element_type=jnp.float32)
    dscore_bf = (prob * (dprob - delta)).astype(jnp.bfloat16)
    dq_ref[0] = jnp.dot(dscore_bf, keys, preferred_element_type=jnp.float32) * scale
    dk_parts = lax.dot_general(dscore_bf, q, (((0,), (0,)), ((), ())),
                               preferred_element_type=jnp.float32) * scale
    dv_parts = lax.dot_general(prob_bf, g, (((0,), (0,)), ((), ())),
                               preferred_element_type=jnp.float32)
    for e in range(entries):
        pk = dk_parts[e * BLK:(e + 1) * BLK]
        pv = dv_parts[e * BLK:(e + 1) * BLK]
        if rand_lo <= e < rand_hi:
            pk = pk.astype(jnp.bfloat16).astype(jnp.float32)
            pv = pv.astype(jnp.bfloat16).astype(jnp.float32)
        t = tgt_ref[b, e]
        dk_ref[t] = dk_ref[t] + pk
        dv_ref[t] = dv_ref[t] + pv


def attention(src, tgt, ok, q, g, k_all, v_all, *, rand_lo, rand_hi, scale):
    nq, entries = src.shape
    nk = k_all.shape[0]
    kern = functools.partial(attn_kernel, entries=entries, rand_lo=rand_lo, rand_hi=rand_hi, scale=scale)
    blk = lambda b, *_: (b, 0, 0)
    whole = lambda b, *_: (0, 0, 0)
    grid_spec = pltpu.PrefetchScalarGridSpec(
        num_scalar_prefetch=3,
        grid=(nq,),
        in_specs=[
            pl.BlockSpec((1, BLK, HD), blk),
            pl.BlockSpec((1, BLK, HD), blk),
            pl.BlockSpec((nk, BLK, HD), whole),
            pl.BlockSpec((nk, BLK, HD), whole),
        ],
        out_specs=[
            pl.BlockSpec((1, BLK, HD), blk),
            pl.BlockSpec((1, BLK, HD), blk),
            pl.BlockSpec((nk, BLK, HD), whole),
            pl.BlockSpec((nk, BLK, HD), whole),
        ],
    )
    return pl.pallas_call(
        kern,
        grid_spec=grid_spec,
        out_shape=[
            jax.ShapeDtypeStruct((nq, BLK, HD), jnp.bfloat16),
            jax.ShapeDtypeStruct((nq, BLK, HD), jnp.float32),
            jax.ShapeDtypeStruct((nk, BLK, HD), jnp.float32),
            jax.ShapeDtypeStruct((nk, BLK, HD), jnp.float32),
        ],
        compiler_params=pltpu.CompilerParams(dimension_semantics=("arbitrary",), vmem_limit_bytes=48 * 1024 * 1024),
    )(src, tgt, ok, q, g, k_all, v_all)


def ring_gather(value, axis, count):
    fwd = [(i, (i + 1) % count) for i in range(count)]
    bwd = [(i, (i - 1) % count) for i in range(count)]
    prev = lax.ppermute(value, axis, fwd)
    nxt = lax.ppermute(value, axis, bwd)
    half = value.shape[0] // 2
    far = jnp.concatenate(
        [
            lax.ppermute(prev[:half], axis, fwd),
            lax.ppermute(nxt[half:], axis, bwd),
        ]
    )
    return [value, prev, far, nxt]


def ring_reduce(pieces, axis, count):
    fwd = [(i, (i + 1) % count) for i in range(count)]
    bwd = [(i, (i - 1) % count) for i in range(count)]
    own, nxt, far, prev = pieces
    half = own.shape[0] // 2
    bf = lambda x: x.astype(jnp.bfloat16)
    f32 = lambda x: x.astype(jnp.float32)
    got_f = lax.ppermute((bf(nxt[half:]), bf(far[:half])), axis, fwd)
    got_b = lax.ppermute((bf(prev[:half]), bf(far[half:])), axis, bwd)
    late_f = lax.ppermute(bf(nxt[:half] + f32(got_f[1])), axis, fwd)
    late_b = lax.ppermute(bf(prev[half:] + f32(got_b[1])), axis, bwd)
    low = own[:half] + f32(got_b[0]) + f32(late_f)
    high = own[half:] + f32(got_f[0]) + f32(late_b)
    return jnp.concatenate([low, high])


def shards(
    query_in, key_in, value_in, out_grad, query_gain, key_gain, random_blocks, global_blocks
):
    tok_rows, feat_dim = query_in.shape
    heads = feat_dim // HD
    rows = lax.axis_size("y")
    my_row = lax.axis_index("y")
    row_tokens = tok_rows * heads
    row_blocks = row_tokens // BLK
    all_blocks = row_blocks * rows
    scale = HD ** (-0.5)

    def to_head(arrays):
        stacked = jnp.stack(arrays).reshape(len(arrays), tok_rows, heads, HD)
        stacked = stacked.transpose(0, 2, 1, 3)
        moved = lax.all_to_all(stacked, "xc", 1, 1, tiled=True)
        return moved.reshape(len(arrays), row_blocks, BLK, HD)

    vg = to_head([value_in, out_grad])

    query_f = query_in.astype(jnp.float32)
    key_f = key_in.astype(jnp.float32)
    sum_query, sum_key = lax.psum(
        (jnp.sum(query_f * query_f, axis=1), jnp.sum(key_f * key_f, axis=1)), "head"
    )
    query_rms = lax.rsqrt(sum_query / D + EPS)
    key_rms = lax.rsqrt(sum_key / D + EPS)
    query_normed = (query_f * query_rms[:, None] * query_gain[None, :]).astype(jnp.bfloat16)
    key_normed = (key_f * key_rms[:, None] * key_gain[None, :]).astype(jnp.bfloat16)

    kq = to_head([key_normed])
    query_h = to_head([query_normed])[0]
    grad_h = vg[1]

    k_all = jnp.concatenate(ring_gather(kq[0], "y", rows))
    v_all = jnp.concatenate(ring_gather(vg[0], "y", rows))

    block_ids = my_row * row_blocks + jnp.arange(row_blocks, dtype=jnp.int32)
    my_random = lax.dynamic_slice_in_dim(random_blocks.astype(jnp.int32), my_row * row_blocks, row_blocks, 0)
    glob = global_blocks.astype(jnp.int32)
    list_ids = jnp.concatenate(
        [
            block_ids[:, None] - 1,
            block_ids[:, None],
            block_ids[:, None] + 1,
            my_random,
            jnp.broadcast_to(glob[None, :], (row_blocks, GLOB)),
        ],
        axis=1,
    )
    valid = (list_ids >= 0) & (list_ids < all_blocks)
    clipped = jnp.clip(list_ids, 0, all_blocks - 1)
    shift_pos = ((my_row - clipped // row_blocks) % rows) * row_blocks + clipped % row_blocks
    target = ((clipped // row_blocks - my_row) % rows) * row_blocks + clipped % row_blocks
    out_h, dq_h, dk_t, dv_t = attention(
        shift_pos, target, valid.astype(jnp.int32), query_h, grad_h, k_all, v_all,
        rand_lo=3, rand_hi=3 + RAND, scale=scale,
    )

    split = lambda x: [x[d * row_blocks : (d + 1) * row_blocks] for d in range(rows)]

    def to_tokens(arrays):
        stacked = jnp.stack([a.reshape(heads, tok_rows, HD) for a in arrays])
        moved = lax.all_to_all(stacked, "xc", 1, 1, tiled=True)
        return moved.transpose(0, 2, 1, 3).reshape(len(arrays), tok_rows, feat_dim)

    early = to_tokens([out_h, dq_h.astype(jnp.bfloat16)])
    own_k = ring_reduce(split(dk_t), "y", rows)
    own_v = ring_reduce(split(dv_t), "y", rows)

    attn_out = early[0]
    dq_normed = early[1].astype(jnp.float32)
    total_query = lax.psum(jnp.sum(query_f * query_gain[None, :] * dq_normed, axis=1), "head")
    late = to_tokens([own_k.astype(jnp.bfloat16), own_v.astype(jnp.bfloat16)])
    dk_normed = late[0].astype(jnp.float32)
    value_grad = late[1]
    dot_key = jnp.sum(key_f * key_gain[None, :] * dk_normed, axis=1) + 0.0 * total_query[0]
    total_key = lax.psum(dot_key, "head")
    query_grad = (
        query_rms[:, None] * query_gain[None, :] * dq_normed
        - query_f * (query_rms**3 * total_query / D)[:, None]
    ).astype(jnp.bfloat16)
    key_grad = (
        key_rms[:, None] * key_gain[None, :] * dk_normed
        - key_f * (key_rms**3 * total_key / D)[:, None]
    ).astype(jnp.bfloat16)
    return (attn_out, query_grad, key_grad, value_grad)


def solution(mesh):
    seq = mesh.shape["seq"]
    head = mesh.shape["head"]
    row = D // head // HD
    sub = Mesh(mesh.devices.reshape(seq // row, row, head), ("y", "xc", "head"))
    tok = P(("y", "xc"), "head")
    in_specs = (tok, tok, tok, tok, P("head"), P("head"), P(), P())
    out_specs = (tok, tok, tok, tok)
    return jax.shard_map(shards, mesh=sub, in_specs=in_specs, out_specs=out_specs, check_vma=False)
```

```python
import jax
import jax.numpy as jnp
import functools

from jax import lax
from jax.experimental import pallas as pl
from jax.experimental.pallas import tpu as pltpu
from jax.sharding import Mesh

from jax.sharding import PartitionSpec as P

D = 4096
HD = 128
BLK = 64
RAND = 3
GLOB = 2


EPS = 1e-06
NEG = -1e30


def attn_kernel(src_ref, tgt_ref, ok_ref, q_ref, g_ref, k_ref, v_ref,
                o_ref, dq_ref, dk_own_ref, dv_own_ref, dk_far_ref, dv_far_ref, dk_ref, dv_ref,
                *, entries, rand_lo, rand_hi, scale):
    b = pl.program_id(0)
    own_blocks = dk_own_ref.shape[0]

    @pl.when(b == 0)
    def _():
        dk_ref[...] = jnp.zeros_like(dk_ref)
        dv_ref[...] = jnp.zeros_like(dv_ref)

    q = q_ref[0]
    g = g_ref[0]
    keys = jnp.concatenate([k_ref[src_ref[b, e]] for e in range(entries)], axis=0)
    vals = jnp.concatenate([v_ref[src_ref[b, e]] for e in range(entries)], axis=0)
    lane_entry = lax.broadcasted_iota(jnp.int32, (1, entries * BLK), 1) // BLK
    ok = jnp.zeros((1, entries * BLK), jnp.int32)
    for e in range(entries):
        ok = jnp.where(lane_entry == e, ok_ref[b, e], ok)
    scores = lax.dot_general(q, keys, (((1,), (1,)), ((), ())),
                             preferred_element_type=jnp.float32) * scale
    scores = jnp.where(ok > 0, scores, NEG)
    top = jnp.max(scores, axis=1, keepdims=True)
    expd = jnp.exp(scores - top)
    prob = expd / jnp.sum(expd, axis=1, keepdims=True)
    prob_bf = prob.astype(jnp.bfloat16)
    out = jnp.dot(prob_bf, vals, preferred_element_type=jnp.float32).astype(jnp.bfloat16)
    o_ref[0] = out
    delta = jnp.sum(g.astype(jnp.float32) * out.astype(jnp.float32), axis=1, keepdims=True)
    dprob = lax.dot_general(g, vals, (((1,), (1,)), ((), ())),
                            preferred_element_type=jnp.float32)
    dscore_bf = (prob * (dprob - delta)).astype(jnp.bfloat16)
    dq_ref[0] = (jnp.dot(dscore_bf, keys, preferred_element_type=jnp.float32) * scale).astype(jnp.bfloat16)
    dk_parts = lax.dot_general(dscore_bf, q, (((0,), (0,)), ((), ())),
                               preferred_element_type=jnp.float32) * scale
    dv_parts = lax.dot_general(prob_bf, g, (((0,), (0,)), ((), ())),
                               preferred_element_type=jnp.float32)
    for e in range(entries):
        pk = dk_parts[e * BLK:(e + 1) * BLK]
        pv = dv_parts[e * BLK:(e + 1) * BLK]
        if rand_lo <= e < rand_hi:
            pk = pk.astype(jnp.bfloat16).astype(jnp.float32)
            pv = pv.astype(jnp.bfloat16).astype(jnp.float32)
        t = tgt_ref[b, e]
        dk_ref[t] = dk_ref[t] + pk
        dv_ref[t] = dv_ref[t] + pv

    @pl.when(b == pl.num_programs(0) - 1)
    def _():
        dk_own_ref[...] = dk_ref[:own_blocks]
        dv_own_ref[...] = dv_ref[:own_blocks]
        dk_far_ref[...] = dk_ref[own_blocks:].astype(jnp.bfloat16)
        dv_far_ref[...] = dv_ref[own_blocks:].astype(jnp.bfloat16)


def attention(src, tgt, ok, q, g, k_all, v_all, *, rand_lo, rand_hi, scale):
    nq, entries = src.shape
    nk = k_all.shape[0]
    kern = functools.partial(attn_kernel, entries=entries, rand_lo=rand_lo, rand_hi=rand_hi, scale=scale)
    blk = lambda b, *_: (b, 0, 0)
    whole = lambda b, *_: (0, 0, 0)
    grid_spec = pltpu.PrefetchScalarGridSpec(
        num_scalar_prefetch=3,
        grid=(nq,),
        in_specs=[
            pl.BlockSpec((1, BLK, HD), blk),
            pl.BlockSpec((1, BLK, HD), blk),
            pl.BlockSpec((nk, BLK, HD), whole),
            pl.BlockSpec((nk, BLK, HD), whole),
        ],
        out_specs=[
            pl.BlockSpec((1, BLK, HD), blk),
            pl.BlockSpec((1, BLK, HD), blk),
            pl.BlockSpec((nq, BLK, HD), whole),
            pl.BlockSpec((nq, BLK, HD), whole),
            pl.BlockSpec((nk - nq, BLK, HD), whole),
            pl.BlockSpec((nk - nq, BLK, HD), whole),
        ],
        scratch_shapes=[
            pltpu.VMEM((nk, BLK, HD), jnp.float32),
            pltpu.VMEM((nk, BLK, HD), jnp.float32),
        ],
    )
    return pl.pallas_call(
        kern,
        grid_spec=grid_spec,
        out_shape=[
            jax.ShapeDtypeStruct((nq, BLK, HD), jnp.bfloat16),
            jax.ShapeDtypeStruct((nq, BLK, HD), jnp.bfloat16),
            jax.ShapeDtypeStruct((nq, BLK, HD), jnp.float32),
            jax.ShapeDtypeStruct((nq, BLK, HD), jnp.float32),
            jax.ShapeDtypeStruct((nk - nq, BLK, HD), jnp.bfloat16),
            jax.ShapeDtypeStruct((nk - nq, BLK, HD), jnp.bfloat16),
        ],
        compiler_params=pltpu.CompilerParams(dimension_semantics=("arbitrary",), vmem_limit_bytes=48 * 1024 * 1024),
    )(src, tgt, ok, q, g, k_all, v_all)


def head_sum(value, axis):
    count = lax.axis_size(axis)
    if count & (count - 1):
        return lax.psum(value, axis)
    step = 1
    while step < count:
        value = value + lax.ppermute(value, axis, [(i, i ^ step) for i in range(count)])
        step *= 2
    return value


def ring_gather(value, axis, count):
    fwd = [(i, (i + 1) % count) for i in range(count)]
    bwd = [(i, (i - 1) % count) for i in range(count)]
    prev = lax.ppermute(value, axis, fwd)
    nxt = lax.ppermute(value, axis, bwd)
    half = value.shape[0] // 2
    far = jnp.concatenate(
        [
            lax.ppermute(prev[:half], axis, fwd),
            lax.ppermute(nxt[half:], axis, bwd),
        ]
    )
    return [value, prev, far, nxt]


def ring_reduce(pieces, axis, count):
    fwd = [(i, (i + 1) % count) for i in range(count)]
    bwd = [(i, (i - 1) % count) for i in range(count)]
    own, nxt, far, prev = pieces
    half = own.shape[0] // 2
    bf = lambda x: x.astype(jnp.bfloat16)
    f32 = lambda x: x.astype(jnp.float32)
    got_f = lax.ppermute((bf(nxt[half:]), bf(far[:half])), axis, fwd)
    got_b = lax.ppermute((bf(prev[:half]), bf(far[half:])), axis, bwd)
    late_f = lax.ppermute(bf(nxt[:half] + f32(got_f[1])), axis, fwd)
    late_b = lax.ppermute(bf(prev[half:] + f32(got_b[1])), axis, bwd)
    low = own[:half] + f32(got_b[0]) + f32(late_f)
    high = own[half:] + f32(got_f[0]) + f32(late_b)
    return jnp.concatenate([low, high])


def shards(
    query_in, key_in, value_in, out_grad, query_gain, key_gain, random_blocks, global_blocks
):
    tok_rows, feat_dim = query_in.shape
    heads = feat_dim // HD
    rows = lax.axis_size("y")
    my_row = lax.axis_index("y")
    row_tokens = tok_rows * heads
    row_blocks = row_tokens // BLK
    all_blocks = row_blocks * rows
    scale = HD ** (-0.5)

    def to_head(arrays):
        stacked = jnp.stack(arrays).reshape(len(arrays), tok_rows, heads, HD)
        stacked = stacked.transpose(0, 2, 1, 3)
        moved = lax.all_to_all(stacked, "xc", 1, 1, tiled=True)
        return moved.reshape(len(arrays), row_blocks, BLK, HD)

    vg = to_head([value_in, out_grad])

    query_f = query_in.astype(jnp.float32)
    key_f = key_in.astype(jnp.float32)
    sums = head_sum(jnp.stack([jnp.sum(query_f * query_f, axis=1), jnp.sum(key_f * key_f, axis=1)]), "head")
    sum_query, sum_key = sums[0], sums[1]
    query_rms = lax.rsqrt(sum_query / D + EPS)
    key_rms = lax.rsqrt(sum_key / D + EPS)
    query_normed = (query_f * query_rms[:, None] * query_gain[None, :]).astype(jnp.bfloat16)
    key_normed = (key_f * key_rms[:, None] * key_gain[None, :]).astype(jnp.bfloat16)

    kq = to_head([key_normed])
    query_h = to_head([query_normed])[0]
    grad_h = vg[1]

    k_all = jnp.concatenate(ring_gather(kq[0], "y", rows))
    v_all = jnp.concatenate(ring_gather(vg[0], "y", rows))

    block_ids = my_row * row_blocks + jnp.arange(row_blocks, dtype=jnp.int32)
    my_random = lax.dynamic_slice_in_dim(random_blocks.astype(jnp.int32), my_row * row_blocks, row_blocks, 0)
    glob = global_blocks.astype(jnp.int32)
    list_ids = jnp.concatenate(
        [
            block_ids[:, None] - 1,
            block_ids[:, None],
            block_ids[:, None] + 1,
            my_random,
            jnp.broadcast_to(glob[None, :], (row_blocks, GLOB)),
        ],
        axis=1,
    )
    valid = (list_ids >= 0) & (list_ids < all_blocks)
    clipped = jnp.clip(list_ids, 0, all_blocks - 1)
    shift_pos = ((my_row - clipped // row_blocks) % rows) * row_blocks + clipped % row_blocks
    target = ((clipped // row_blocks - my_row) % rows) * row_blocks + clipped % row_blocks
    out_h, dq_h, dk_own, dv_own, dk_far, dv_far = attention(
        shift_pos, target, valid.astype(jnp.int32), query_h, grad_h, k_all, v_all,
        rand_lo=3, rand_hi=3 + RAND, scale=scale,
    )

    split = lambda own, far: [own] + [far[d * row_blocks : (d + 1) * row_blocks] for d in range(rows - 1)]

    def to_tokens(arrays):
        stacked = jnp.stack([a.reshape(heads, tok_rows, HD) for a in arrays])
        moved = lax.all_to_all(stacked, "xc", 1, 1, tiled=True)
        return moved.transpose(0, 2, 1, 3).reshape(len(arrays), tok_rows, feat_dim)

    early = to_tokens([out_h, dq_h])
    own_k = ring_reduce(split(dk_own, dk_far), "y", rows)
    own_v = ring_reduce(split(dv_own, dv_far), "y", rows)

    attn_out = early[0]
    dq_normed = early[1].astype(jnp.float32)
    total_query = head_sum(jnp.sum(query_f * query_gain[None, :] * dq_normed, axis=1), "head")
    late = to_tokens([own_k.astype(jnp.bfloat16), own_v.astype(jnp.bfloat16)])
    dk_normed = late[0].astype(jnp.float32)
    value_grad = late[1]
    total_key = head_sum(jnp.sum(key_f * key_gain[None, :] * dk_normed, axis=1), "head")
    query_grad = (
        query_rms[:, None] * query_gain[None, :] * dq_normed
        - query_f * (query_rms**3 * total_query / D)[:, None]
    ).astype(jnp.bfloat16)
    key_grad = (
        key_rms[:, None] * key_gain[None, :] * dk_normed
        - key_f * (key_rms**3 * total_key / D)[:, None]
    ).astype(jnp.bfloat16)
    return (attn_out, query_grad, key_grad, value_grad)


def solution(mesh):
    seq = mesh.shape["seq"]
    head = mesh.shape["head"]
    row = D // head // HD
    sub = Mesh(mesh.devices.reshape(seq // row, row, head), ("y", "xc", "head"))
    tok = P(("y", "xc"), "head")
    in_specs = (tok, tok, tok, tok, P("head"), P("head"), P(), P())
    out_specs = (tok, tok, tok, tok)
    return jax.shard_map(shards, mesh=sub, in_specs=in_specs, out_specs=out_specs, check_vma=False)
```

```python
import jax
import jax.numpy as jnp
import functools

from jax import lax
from jax.experimental import pallas as pl
from jax.experimental.pallas import tpu as pltpu
from jax.sharding import Mesh

from jax.sharding import PartitionSpec as P

D = 4096
HD = 128
BLK = 64
RAND = 3
GLOB = 2


EPS = 1e-06
NEG = -1e30


def attn_kernel(src_ref, tgt_ref, ok_ref, q_ref, g_ref, k_ref, v_ref,
                o_ref, dq_ref, dk_own_ref, dv_own_ref, dk_far_ref, dv_far_ref, dk_ref, dv_ref,
                *, entries, rand_lo, rand_hi, scale, group):
    step = pl.program_id(0)
    own_blocks = dk_own_ref.shape[0]

    @pl.when(step == 0)
    def _():
        dk_ref[...] = jnp.zeros_like(dk_ref)
        dv_ref[...] = jnp.zeros_like(dv_ref)

    lane_entry = lax.broadcasted_iota(jnp.int32, (1, entries * BLK), 1) // BLK
    for i in range(group):
        b = step * group + i
        q = q_ref[i]
        g = g_ref[i]
        keys = jnp.concatenate([k_ref[src_ref[b, e]] for e in range(entries)], axis=0)
        vals = jnp.concatenate([v_ref[src_ref[b, e]] for e in range(entries)], axis=0)
        ok = jnp.zeros((1, entries * BLK), jnp.int32)
        for e in range(entries):
            ok = jnp.where(lane_entry == e, ok_ref[b, e], ok)
        scores = lax.dot_general(q, keys, (((1,), (1,)), ((), ())),
                                 preferred_element_type=jnp.float32) * scale
        scores = jnp.where(ok > 0, scores, NEG)
        top = jnp.max(scores, axis=1, keepdims=True)
        expd = jnp.exp(scores - top)
        prob = expd / jnp.sum(expd, axis=1, keepdims=True)
        prob_bf = prob.astype(jnp.bfloat16)
        out = jnp.dot(prob_bf, vals, preferred_element_type=jnp.float32).astype(jnp.bfloat16)
        o_ref[i] = out
        delta = jnp.sum(g.astype(jnp.float32) * out.astype(jnp.float32), axis=1, keepdims=True)
        dprob = lax.dot_general(g, vals, (((1,), (1,)), ((), ())),
                                preferred_element_type=jnp.float32)
        dscore_bf = (prob * (dprob - delta)).astype(jnp.bfloat16)
        dq_ref[i] = (jnp.dot(dscore_bf, keys, preferred_element_type=jnp.float32) * scale).astype(jnp.bfloat16)
        dk_parts = lax.dot_general(dscore_bf, q, (((0,), (0,)), ((), ())),
                                   preferred_element_type=jnp.float32) * scale
        dv_parts = lax.dot_general(prob_bf, g, (((0,), (0,)), ((), ())),
                                   preferred_element_type=jnp.float32)
        for e in range(entries):
            pk = dk_parts[e * BLK:(e + 1) * BLK]
            pv = dv_parts[e * BLK:(e + 1) * BLK]
            if rand_lo <= e < rand_hi:
                pk = pk.astype(jnp.bfloat16).astype(jnp.float32)
                pv = pv.astype(jnp.bfloat16).astype(jnp.float32)
            t = tgt_ref[b, e]
            dk_ref[t] = dk_ref[t] + pk
            dv_ref[t] = dv_ref[t] + pv

    @pl.when(step == pl.num_programs(0) - 1)
    def _():
        dk_own_ref[...] = dk_ref[:own_blocks]
        dv_own_ref[...] = dv_ref[:own_blocks]
        dk_far_ref[...] = dk_ref[own_blocks:].astype(jnp.bfloat16)
        dv_far_ref[...] = dv_ref[own_blocks:].astype(jnp.bfloat16)


def attention(src, tgt, ok, q, g, k_all, v_all, *, rand_lo, rand_hi, scale, group=4):
    nq, entries = src.shape
    nk = k_all.shape[0]
    kern = functools.partial(attn_kernel, entries=entries, rand_lo=rand_lo, rand_hi=rand_hi,
                             scale=scale, group=group)
    blk = lambda b, *_: (b, 0, 0)
    whole = lambda b, *_: (0, 0, 0)
    grid_spec = pltpu.PrefetchScalarGridSpec(
        num_scalar_prefetch=3,
        grid=(nq // group,),
        in_specs=[
            pl.BlockSpec((group, BLK, HD), blk),
            pl.BlockSpec((group, BLK, HD), blk),
            pl.BlockSpec((nk, BLK, HD), whole),
            pl.BlockSpec((nk, BLK, HD), whole),
        ],
        out_specs=[
            pl.BlockSpec((group, BLK, HD), blk),
            pl.BlockSpec((group, BLK, HD), blk),
            pl.BlockSpec((nq, BLK, HD), whole),
            pl.BlockSpec((nq, BLK, HD), whole),
            pl.BlockSpec((nk - nq, BLK, HD), whole),
            pl.BlockSpec((nk - nq, BLK, HD), whole),
        ],
        scratch_shapes=[
            pltpu.VMEM((nk, BLK, HD), jnp.float32),
            pltpu.VMEM((nk, BLK, HD), jnp.float32),
        ],
    )
    return pl.pallas_call(
        kern,
        grid_spec=grid_spec,
        out_shape=[
            jax.ShapeDtypeStruct((nq, BLK, HD), jnp.bfloat16),
            jax.ShapeDtypeStruct((nq, BLK, HD), jnp.bfloat16),
            jax.ShapeDtypeStruct((nq, BLK, HD), jnp.float32),
            jax.ShapeDtypeStruct((nq, BLK, HD), jnp.float32),
            jax.ShapeDtypeStruct((nk - nq, BLK, HD), jnp.bfloat16),
            jax.ShapeDtypeStruct((nk - nq, BLK, HD), jnp.bfloat16),
        ],
        compiler_params=pltpu.CompilerParams(dimension_semantics=("arbitrary",), vmem_limit_bytes=48 * 1024 * 1024),
    )(src, tgt, ok, q, g, k_all, v_all)


def head_sum(value, axis):
    count = lax.axis_size(axis)
    if count & (count - 1):
        return lax.psum(value, axis)
    step = 1
    while step < count:
        value = value + lax.ppermute(value, axis, [(i, i ^ step) for i in range(count)])
        step *= 2
    return value


def ring_gather(value, axis, count):
    fwd = [(i, (i + 1) % count) for i in range(count)]
    bwd = [(i, (i - 1) % count) for i in range(count)]
    prev = lax.ppermute(value, axis, fwd)
    nxt = lax.ppermute(value, axis, bwd)
    half = value.shape[0] // 2
    far = jnp.concatenate(
        [
            lax.ppermute(prev[:half], axis, fwd),
            lax.ppermute(nxt[half:], axis, bwd),
        ]
    )
    return [value, prev, far, nxt]


def ring_reduce(pieces, axis, count):
    fwd = [(i, (i + 1) % count) for i in range(count)]
    bwd = [(i, (i - 1) % count) for i in range(count)]
    own, nxt, far, prev = pieces
    half = own.shape[0] // 2
    bf = lambda x: x.astype(jnp.bfloat16)
    f32 = lambda x: x.astype(jnp.float32)
    got_f = lax.ppermute((bf(nxt[half:]), bf(far[:half])), axis, fwd)
    got_b = lax.ppermute((bf(prev[:half]), bf(far[half:])), axis, bwd)
    late_f = lax.ppermute(bf(nxt[:half] + f32(got_f[1])), axis, fwd)
    late_b = lax.ppermute(bf(prev[half:] + f32(got_b[1])), axis, bwd)
    low = own[:half] + f32(got_b[0]) + f32(late_f)
    high = own[half:] + f32(got_f[0]) + f32(late_b)
    return jnp.concatenate([low, high])


def shards(
    query_in, key_in, value_in, out_grad, query_gain, key_gain, random_blocks, global_blocks
):
    tok_rows, feat_dim = query_in.shape
    heads = feat_dim // HD
    rows = lax.axis_size("y")
    my_row = lax.axis_index("y")
    row_tokens = tok_rows * heads
    row_blocks = row_tokens // BLK
    all_blocks = row_blocks * rows
    scale = HD ** (-0.5)

    def to_head(arrays):
        stacked = jnp.stack(arrays).reshape(len(arrays), tok_rows, heads, HD)
        stacked = stacked.transpose(0, 2, 1, 3)
        moved = lax.all_to_all(stacked, "xc", 1, 1, tiled=True)
        return moved.reshape(len(arrays), row_blocks, BLK, HD)

    vg = to_head([value_in, out_grad])

    query_f = query_in.astype(jnp.float32)
    key_f = key_in.astype(jnp.float32)
    after = 0.0 * vg[0, 0, 0, 0].astype(jnp.float32)
    sums = head_sum(jnp.stack([jnp.sum(query_f * query_f, axis=1), jnp.sum(key_f * key_f, axis=1)]) + after, "head")
    sum_query, sum_key = sums[0], sums[1]
    query_rms = lax.rsqrt(sum_query / D + EPS)
    key_rms = lax.rsqrt(sum_key / D + EPS)
    query_normed = (query_f * query_rms[:, None] * query_gain[None, :]).astype(jnp.bfloat16)
    key_normed = (key_f * key_rms[:, None] * key_gain[None, :]).astype(jnp.bfloat16)

    kq = to_head([key_normed])
    query_h = to_head([query_normed])[0]
    grad_h = vg[1]

    k_all = jnp.concatenate(ring_gather(kq[0], "y", rows))
    v_all = jnp.concatenate(ring_gather(vg[0], "y", rows))

    block_ids = my_row * row_blocks + jnp.arange(row_blocks, dtype=jnp.int32)
    my_random = lax.dynamic_slice_in_dim(random_blocks.astype(jnp.int32), my_row * row_blocks, row_blocks, 0)
    glob = global_blocks.astype(jnp.int32)
    list_ids = jnp.concatenate(
        [
            block_ids[:, None] - 1,
            block_ids[:, None],
            block_ids[:, None] + 1,
            my_random,
            jnp.broadcast_to(glob[None, :], (row_blocks, GLOB)),
        ],
        axis=1,
    )
    valid = (list_ids >= 0) & (list_ids < all_blocks)
    clipped = jnp.clip(list_ids, 0, all_blocks - 1)
    shift_pos = ((my_row - clipped // row_blocks) % rows) * row_blocks + clipped % row_blocks
    target = ((clipped // row_blocks - my_row) % rows) * row_blocks + clipped % row_blocks
    out_h, dq_h, dk_own, dv_own, dk_far, dv_far = attention(
        shift_pos, target, valid.astype(jnp.int32), query_h, grad_h, k_all, v_all,
        rand_lo=3, rand_hi=3 + RAND, scale=scale,
    )

    split = lambda own, far: [own] + [far[d * row_blocks : (d + 1) * row_blocks] for d in range(rows - 1)]

    def to_tokens(arrays):
        stacked = jnp.stack([a.reshape(heads, tok_rows, HD) for a in arrays])
        moved = lax.all_to_all(stacked, "xc", 1, 1, tiled=True)
        return moved.transpose(0, 2, 1, 3).reshape(len(arrays), tok_rows, feat_dim)

    early = to_tokens([out_h, dq_h])
    own_k = ring_reduce(split(dk_own, dk_far), "y", rows)
    own_v = ring_reduce(split(dv_own, dv_far), "y", rows)

    attn_out = early[0]
    dq_normed = early[1].astype(jnp.float32)
    total_query = head_sum(jnp.sum(query_f * query_gain[None, :] * dq_normed, axis=1), "head")
    late = to_tokens([own_k.astype(jnp.bfloat16), own_v.astype(jnp.bfloat16)])
    dk_normed = late[0].astype(jnp.float32)
    value_grad = late[1]
    total_key = head_sum(jnp.sum(key_f * key_gain[None, :] * dk_normed, axis=1), "head")
    query_grad = (
        query_rms[:, None] * query_gain[None, :] * dq_normed
        - query_f * (query_rms**3 * total_query / D)[:, None]
    ).astype(jnp.bfloat16)
    key_grad = (
        key_rms[:, None] * key_gain[None, :] * dk_normed
        - key_f * (key_rms**3 * total_key / D)[:, None]
    ).astype(jnp.bfloat16)
    return (attn_out, query_grad, key_grad, value_grad)


def solution(mesh):
    seq = mesh.shape["seq"]
    head = mesh.shape["head"]
    row = D // head // HD
    sub = Mesh(mesh.devices.reshape(seq // row, row, head), ("y", "xc", "head"))
    tok = P(("y", "xc"), "head")
    in_specs = (tok, tok, tok, tok, P("head"), P("head"), P(), P())
    out_specs = (tok, tok, tok, tok)
    return jax.shard_map(shards, mesh=sub, in_specs=in_specs, out_specs=out_specs, check_vma=False)
```

```python
import jax
import jax.numpy as jnp
import functools

from jax import lax
from jax.experimental import pallas as pl
from jax.experimental.pallas import tpu as pltpu
from jax.sharding import Mesh

from jax.sharding import PartitionSpec as P

D = 4096
HD = 128
BLK = 64
RAND = 3
GLOB = 2


EPS = 1e-06
NEG = -1e30


def attn_kernel(src_ref, tgt_ref, ok_ref, q_ref, g_ref, k_ref, v_ref,
                o_ref, dq_ref, dk_own_ref, dv_own_ref, dk_far_ref, dv_far_ref, dk_ref, dv_ref,
                *, entries, rand_lo, rand_hi, scale, group):
    step = pl.program_id(0)
    own_blocks = dk_own_ref.shape[0]

    @pl.when(step == 0)
    def _():
        dk_ref[...] = jnp.zeros_like(dk_ref)
        dv_ref[...] = jnp.zeros_like(dv_ref)

    lane_entry = lax.broadcasted_iota(jnp.int32, (1, entries * BLK), 1) // BLK
    for i in range(group):
        b = step * group + i
        q = q_ref[i]
        g = g_ref[i]
        keys = jnp.concatenate([k_ref[src_ref[b, e]] for e in range(entries)], axis=0)
        vals = jnp.concatenate([v_ref[src_ref[b, e]] for e in range(entries)], axis=0)
        ok = jnp.zeros((1, entries * BLK), jnp.int32)
        for e in range(entries):
            ok = jnp.where(lane_entry == e, ok_ref[b, e], ok)
        scores = lax.dot_general(q, keys, (((1,), (1,)), ((), ())),
                                 preferred_element_type=jnp.float32) * scale
        scores = jnp.where(ok > 0, scores, NEG)
        top = jnp.max(scores, axis=1, keepdims=True)
        expd = jnp.exp(scores - top)
        prob = expd / jnp.sum(expd, axis=1, keepdims=True)
        prob_bf = prob.astype(jnp.bfloat16)
        out = jnp.dot(prob_bf, vals, preferred_element_type=jnp.float32).astype(jnp.bfloat16)
        o_ref[i] = out
        delta = jnp.sum(g.astype(jnp.float32) * out.astype(jnp.float32), axis=1, keepdims=True)
        dprob = lax.dot_general(g, vals, (((1,), (1,)), ((), ())),
                                preferred_element_type=jnp.float32)
        dscore_bf = (prob * (dprob - delta)).astype(jnp.bfloat16)
        dq_ref[i] = (jnp.dot(dscore_bf, keys, preferred_element_type=jnp.float32) * scale).astype(jnp.bfloat16)
        dk_parts = lax.dot_general(dscore_bf, q, (((0,), (0,)), ((), ())),
                                   preferred_element_type=jnp.float32) * scale
        dv_parts = lax.dot_general(prob_bf, g, (((0,), (0,)), ((), ())),
                                   preferred_element_type=jnp.float32)
        for e in range(entries):
            pk = dk_parts[e * BLK:(e + 1) * BLK]
            pv = dv_parts[e * BLK:(e + 1) * BLK]
            if rand_lo <= e < rand_hi:
                pk = pk.astype(jnp.bfloat16).astype(jnp.float32)
                pv = pv.astype(jnp.bfloat16).astype(jnp.float32)
            t = tgt_ref[b, e]
            dk_ref[t] = dk_ref[t] + pk
            dv_ref[t] = dv_ref[t] + pv

    @pl.when(step == pl.num_programs(0) - 1)
    def _():
        dk_own_ref[...] = dk_ref[:own_blocks]
        dv_own_ref[...] = dv_ref[:own_blocks]
        dk_far_ref[...] = dk_ref[own_blocks:].astype(jnp.bfloat16)
        dv_far_ref[...] = dv_ref[own_blocks:].astype(jnp.bfloat16)


def attention(src, tgt, ok, q, g, k_all, v_all, *, rand_lo, rand_hi, scale, group=4):
    nq, entries = src.shape
    nk = k_all.shape[0]
    kern = functools.partial(attn_kernel, entries=entries, rand_lo=rand_lo, rand_hi=rand_hi,
                             scale=scale, group=group)
    blk = lambda b, *_: (b, 0, 0)
    whole = lambda b, *_: (0, 0, 0)
    grid_spec = pltpu.PrefetchScalarGridSpec(
        num_scalar_prefetch=3,
        grid=(nq // group,),
        in_specs=[
            pl.BlockSpec((group, BLK, HD), blk),
            pl.BlockSpec((group, BLK, HD), blk),
            pl.BlockSpec((nk, BLK, HD), whole),
            pl.BlockSpec((nk, BLK, HD), whole),
        ],
        out_specs=[
            pl.BlockSpec((group, BLK, HD), blk),
            pl.BlockSpec((group, BLK, HD), blk),
            pl.BlockSpec((nq, BLK, HD), whole),
            pl.BlockSpec((nq, BLK, HD), whole),
            pl.BlockSpec((nk - nq, BLK, HD), whole),
            pl.BlockSpec((nk - nq, BLK, HD), whole),
        ],
        scratch_shapes=[
            pltpu.VMEM((nk, BLK, HD), jnp.float32),
            pltpu.VMEM((nk, BLK, HD), jnp.float32),
        ],
    )
    return pl.pallas_call(
        kern,
        grid_spec=grid_spec,
        out_shape=[
            jax.ShapeDtypeStruct((nq, BLK, HD), jnp.bfloat16),
            jax.ShapeDtypeStruct((nq, BLK, HD), jnp.bfloat16),
            jax.ShapeDtypeStruct((nq, BLK, HD), jnp.float32),
            jax.ShapeDtypeStruct((nq, BLK, HD), jnp.float32),
            jax.ShapeDtypeStruct((nk - nq, BLK, HD), jnp.bfloat16),
            jax.ShapeDtypeStruct((nk - nq, BLK, HD), jnp.bfloat16),
        ],
        compiler_params=pltpu.CompilerParams(dimension_semantics=("arbitrary",), vmem_limit_bytes=48 * 1024 * 1024),
    )(src, tgt, ok, q, g, k_all, v_all)


def head_sum(value, axis):
    count = lax.axis_size(axis)
    if count & (count - 1):
        return lax.psum(value, axis)
    step = 1
    while step < count:
        value = value + lax.ppermute(value, axis, [(i, i ^ step) for i in range(count)])
        step *= 2
    return value


def ring_gather(value, axis, count):
    fwd = [(i, (i + 1) % count) for i in range(count)]
    bwd = [(i, (i - 1) % count) for i in range(count)]
    prev = lax.ppermute(value, axis, fwd)
    nxt = lax.ppermute(value, axis, bwd)
    half = value.shape[0] // 2
    far = jnp.concatenate(
        [
            lax.ppermute(prev[:half], axis, fwd),
            lax.ppermute(nxt[half:], axis, bwd),
        ]
    )
    return [value, prev, far, nxt]


def ring_reduce(pieces, axis, count):
    fwd = [(i, (i + 1) % count) for i in range(count)]
    bwd = [(i, (i - 1) % count) for i in range(count)]
    own, nxt, far, prev = pieces
    half = own.shape[0] // 2
    bf = lambda x: x.astype(jnp.bfloat16)
    f32 = lambda x: x.astype(jnp.float32)
    got_f = lax.ppermute((bf(nxt[half:]), bf(far[:half])), axis, fwd)
    got_b = lax.ppermute((bf(prev[:half]), bf(far[half:])), axis, bwd)
    late_f = lax.ppermute(bf(nxt[:half] + f32(got_f[1])), axis, fwd)
    late_b = lax.ppermute(bf(prev[half:] + f32(got_b[1])), axis, bwd)
    low = own[:half] + f32(got_b[0]) + f32(late_f)
    high = own[half:] + f32(got_f[0]) + f32(late_b)
    return jnp.concatenate([low, high])


def shards(
    query_in, key_in, value_in, out_grad, query_gain, key_gain, random_blocks, global_blocks
):
    tok_rows, feat_dim = query_in.shape
    heads = feat_dim // HD
    rows = lax.axis_size("y")
    my_row = lax.axis_index("y")
    row_tokens = tok_rows * heads
    row_blocks = row_tokens // BLK
    all_blocks = row_blocks * rows
    scale = HD ** (-0.5)

    def to_head(arrays):
        stacked = jnp.stack(arrays).reshape(len(arrays), tok_rows, heads, HD)
        stacked = stacked.transpose(0, 2, 1, 3)
        moved = lax.all_to_all(stacked, "xc", 1, 1, tiled=True)
        return moved.reshape(len(arrays), row_blocks, BLK, HD)

    v_rows = ring_gather(value_in, "y", rows)
    vg = to_head(v_rows + [out_grad])
    v_all = vg[:rows].reshape(rows * row_blocks, BLK, HD)
    grad_h = vg[rows]

    query_f = query_in.astype(jnp.float32)
    key_f = key_in.astype(jnp.float32)
    sums = head_sum(jnp.stack([jnp.sum(query_f * query_f, axis=1), jnp.sum(key_f * key_f, axis=1)]), "head")
    sum_query, sum_key = sums[0], sums[1]
    query_rms = lax.rsqrt(sum_query / D + EPS)
    key_rms = lax.rsqrt(sum_key / D + EPS)
    query_normed = (query_f * query_rms[:, None] * query_gain[None, :]).astype(jnp.bfloat16)
    key_normed = (key_f * key_rms[:, None] * key_gain[None, :]).astype(jnp.bfloat16)

    kq = to_head([key_normed, query_normed])
    query_h = kq[1]

    k_all = jnp.concatenate(ring_gather(kq[0], "y", rows))

    block_ids = my_row * row_blocks + jnp.arange(row_blocks, dtype=jnp.int32)
    my_random = lax.dynamic_slice_in_dim(random_blocks.astype(jnp.int32), my_row * row_blocks, row_blocks, 0)
    glob = global_blocks.astype(jnp.int32)
    list_ids = jnp.concatenate(
        [
            block_ids[:, None] - 1,
            block_ids[:, None],
            block_ids[:, None] + 1,
            my_random,
            jnp.broadcast_to(glob[None, :], (row_blocks, GLOB)),
        ],
        axis=1,
    )
    valid = (list_ids >= 0) & (list_ids < all_blocks)
    clipped = jnp.clip(list_ids, 0, all_blocks - 1)
    shift_pos = ((my_row - clipped // row_blocks) % rows) * row_blocks + clipped % row_blocks
    target = ((clipped // row_blocks - my_row) % rows) * row_blocks + clipped % row_blocks
    out_h, dq_h, dk_own, dv_own, dk_far, dv_far = attention(
        shift_pos, target, valid.astype(jnp.int32), query_h, grad_h, k_all, v_all,
        rand_lo=3, rand_hi=3 + RAND, scale=scale,
    )

    split = lambda own, far: [own] + [far[d * row_blocks : (d + 1) * row_blocks] for d in range(rows - 1)]

    def to_tokens(arrays):
        stacked = jnp.stack([a.reshape(heads, tok_rows, HD) for a in arrays])
        moved = lax.all_to_all(stacked, "xc", 1, 1, tiled=True)
        return moved.transpose(0, 2, 1, 3).reshape(len(arrays), tok_rows, feat_dim)

    early = to_tokens([out_h, dq_h])
    own_k = ring_reduce(split(dk_own, dk_far), "y", rows)
    own_v = ring_reduce(split(dv_own, dv_far), "y", rows)

    attn_out = early[0]
    dq_normed = early[1].astype(jnp.float32)
    total_query = head_sum(jnp.sum(query_f * query_gain[None, :] * dq_normed, axis=1), "head")
    late = to_tokens([own_k.astype(jnp.bfloat16), own_v.astype(jnp.bfloat16)])
    dk_normed = late[0].astype(jnp.float32)
    value_grad = late[1]
    total_key = head_sum(jnp.sum(key_f * key_gain[None, :] * dk_normed, axis=1), "head")
    query_grad = (
        query_rms[:, None] * query_gain[None, :] * dq_normed
        - query_f * (query_rms**3 * total_query / D)[:, None]
    ).astype(jnp.bfloat16)
    key_grad = (
        key_rms[:, None] * key_gain[None, :] * dk_normed
        - key_f * (key_rms**3 * total_key / D)[:, None]
    ).astype(jnp.bfloat16)
    return (attn_out, query_grad, key_grad, value_grad)


def solution(mesh):
    seq = mesh.shape["seq"]
    head = mesh.shape["head"]
    row = D // head // HD
    sub = Mesh(mesh.devices.reshape(seq // row, row, head), ("y", "xc", "head"))
    tok = P(("y", "xc"), "head")
    in_specs = (tok, tok, tok, tok, P("head"), P("head"), P(), P())
    out_specs = (tok, tok, tok, tok)
    return jax.shard_map(shards, mesh=sub, in_specs=in_specs, out_specs=out_specs, check_vma=False)
```

```python
import jax
import jax.numpy as jnp
import functools

from jax import lax
from jax.experimental import pallas as pl
from jax.experimental.pallas import tpu as pltpu
from jax.sharding import Mesh

from jax.sharding import PartitionSpec as P

D = 4096
HD = 128
BLK = 64
RAND = 3
GLOB = 2


EPS = 1e-06
NEG = -1e30


def attn_kernel(src_ref, tgt_ref, ok_ref, q_ref, g_ref, k_ref, v_ref,
                o_ref, dq_ref, dk_own_ref, dv_own_ref, dk_far_ref, dv_far_ref, dk_ref, dv_ref,
                *, entries, rand_lo, rand_hi, scale, group):
    step = pl.program_id(0)
    own_blocks = dk_own_ref.shape[0]

    @pl.when(step == 0)
    def _():
        dk_ref[...] = jnp.zeros_like(dk_ref)
        dv_ref[...] = jnp.zeros_like(dv_ref)

    lane_entry = lax.broadcasted_iota(jnp.int32, (1, entries * BLK), 1) // BLK
    for i in range(group):
        b = step * group + i
        q = q_ref[i]
        g = g_ref[i]
        keys = jnp.concatenate([k_ref[src_ref[b, e]] for e in range(entries)], axis=0)
        vals = jnp.concatenate([v_ref[src_ref[b, e]] for e in range(entries)], axis=0)
        ok = jnp.zeros((1, entries * BLK), jnp.int32)
        for e in range(entries):
            ok = jnp.where(lane_entry == e, ok_ref[b, e], ok)
        scores = lax.dot_general(q, keys, (((1,), (1,)), ((), ())),
                                 preferred_element_type=jnp.float32) * scale
        scores = jnp.where(ok > 0, scores, NEG)
        top = jnp.max(scores, axis=1, keepdims=True)
        expd = jnp.exp(scores - top)
        prob = expd / jnp.sum(expd, axis=1, keepdims=True)
        prob_bf = prob.astype(jnp.bfloat16)
        out = jnp.dot(prob_bf, vals, preferred_element_type=jnp.float32).astype(jnp.bfloat16)
        o_ref[i] = out
        delta = jnp.sum(g.astype(jnp.float32) * out.astype(jnp.float32), axis=1, keepdims=True)
        dprob = lax.dot_general(g, vals, (((1,), (1,)), ((), ())),
                                preferred_element_type=jnp.float32)
        dscore_bf = (prob * (dprob - delta)).astype(jnp.bfloat16)
        dq_ref[i] = (jnp.dot(dscore_bf, keys, preferred_element_type=jnp.float32) * scale).astype(jnp.bfloat16)
        dk_parts = lax.dot_general(dscore_bf, q, (((0,), (0,)), ((), ())),
                                   preferred_element_type=jnp.float32) * scale
        dv_parts = lax.dot_general(prob_bf, g, (((0,), (0,)), ((), ())),
                                   preferred_element_type=jnp.float32)
        for e in range(entries):
            pk = dk_parts[e * BLK:(e + 1) * BLK]
            pv = dv_parts[e * BLK:(e + 1) * BLK]
            if rand_lo <= e < rand_hi:
                pk = pk.astype(jnp.bfloat16).astype(jnp.float32)
                pv = pv.astype(jnp.bfloat16).astype(jnp.float32)
            t = tgt_ref[b, e]
            dk_ref[t] = dk_ref[t] + pk
            dv_ref[t] = dv_ref[t] + pv

    @pl.when(step == pl.num_programs(0) - 1)
    def _():
        dk_own_ref[...] = dk_ref[:own_blocks]
        dv_own_ref[...] = dv_ref[:own_blocks]
        dk_far_ref[...] = dk_ref[own_blocks:].astype(jnp.bfloat16)
        dv_far_ref[...] = dv_ref[own_blocks:].astype(jnp.bfloat16)


def attention(src, tgt, ok, q, g, k_all, v_all, *, rand_lo, rand_hi, scale, group=4):
    nq, entries = src.shape
    nk = k_all.shape[0]
    kern = functools.partial(attn_kernel, entries=entries, rand_lo=rand_lo, rand_hi=rand_hi,
                             scale=scale, group=group)
    blk = lambda b, *_: (b, 0, 0)
    whole = lambda b, *_: (0, 0, 0)
    grid_spec = pltpu.PrefetchScalarGridSpec(
        num_scalar_prefetch=3,
        grid=(nq // group,),
        in_specs=[
            pl.BlockSpec((group, BLK, HD), blk),
            pl.BlockSpec((group, BLK, HD), blk),
            pl.BlockSpec((nk, BLK, HD), whole),
            pl.BlockSpec((nk, BLK, HD), whole),
        ],
        out_specs=[
            pl.BlockSpec((group, BLK, HD), blk),
            pl.BlockSpec((group, BLK, HD), blk),
            pl.BlockSpec((nq, BLK, HD), whole),
            pl.BlockSpec((nq, BLK, HD), whole),
            pl.BlockSpec((nk - nq, BLK, HD), whole),
            pl.BlockSpec((nk - nq, BLK, HD), whole),
        ],
        scratch_shapes=[
            pltpu.VMEM((nk, BLK, HD), jnp.float32),
            pltpu.VMEM((nk, BLK, HD), jnp.float32),
        ],
    )
    return pl.pallas_call(
        kern,
        grid_spec=grid_spec,
        out_shape=[
            jax.ShapeDtypeStruct((nq, BLK, HD), jnp.bfloat16),
            jax.ShapeDtypeStruct((nq, BLK, HD), jnp.bfloat16),
            jax.ShapeDtypeStruct((nq, BLK, HD), jnp.float32),
            jax.ShapeDtypeStruct((nq, BLK, HD), jnp.float32),
            jax.ShapeDtypeStruct((nk - nq, BLK, HD), jnp.bfloat16),
            jax.ShapeDtypeStruct((nk - nq, BLK, HD), jnp.bfloat16),
        ],
        compiler_params=pltpu.CompilerParams(dimension_semantics=("arbitrary",), vmem_limit_bytes=48 * 1024 * 1024),
    )(src, tgt, ok, q, g, k_all, v_all)


def head_sum(value, axis):
    count = lax.axis_size(axis)
    if count & (count - 1):
        return lax.psum(value, axis)
    step = 1
    while step < count:
        value = value + lax.ppermute(value, axis, [(i, i ^ step) for i in range(count)])
        step *= 2
    return value


def ring_gather(value, axis, count):
    fwd = [(i, (i + 1) % count) for i in range(count)]
    bwd = [(i, (i - 1) % count) for i in range(count)]
    prev = lax.ppermute(value, axis, fwd)
    nxt = lax.ppermute(value, axis, bwd)
    half = value.shape[0] // 2
    far = jnp.concatenate(
        [
            lax.ppermute(prev[:half], axis, fwd),
            lax.ppermute(nxt[half:], axis, bwd),
        ]
    )
    return [value, prev, far, nxt]


def ring_reduce(pieces, axis, count):
    fwd = [(i, (i + 1) % count) for i in range(count)]
    bwd = [(i, (i - 1) % count) for i in range(count)]
    own, nxt, far, prev = pieces
    half = own.shape[0] // 2
    bf = lambda x: x.astype(jnp.bfloat16)
    f32 = lambda x: x.astype(jnp.float32)
    got_f = lax.ppermute((bf(nxt[half:]), bf(far[:half])), axis, fwd)
    got_b = lax.ppermute((bf(prev[:half]), bf(far[half:])), axis, bwd)
    late_f = lax.ppermute(bf(nxt[:half] + f32(got_f[1])), axis, fwd)
    late_b = lax.ppermute(bf(prev[half:] + f32(got_b[1])), axis, bwd)
    low = own[:half] + f32(got_b[0]) + f32(late_f)
    high = own[half:] + f32(got_f[0]) + f32(late_b)
    return jnp.concatenate([low, high])


def shards(
    query_in, key_in, value_in, out_grad, query_gain, key_gain, random_blocks, global_blocks
):
    tok_rows, feat_dim = query_in.shape
    heads = feat_dim // HD
    rows = lax.axis_size("y")
    my_row = lax.axis_index("y")
    row_tokens = tok_rows * heads
    row_blocks = row_tokens // BLK
    all_blocks = row_blocks * rows
    scale = HD ** (-0.5)

    def to_head(arrays):
        stacked = jnp.stack(arrays).reshape(len(arrays), tok_rows, heads, HD)
        stacked = stacked.transpose(0, 2, 1, 3)
        moved = lax.all_to_all(stacked, "xc", 1, 1, tiled=True)
        return moved.reshape(len(arrays), row_blocks, BLK, HD)

    v_rows = ring_gather(value_in, "y", rows)
    v_all = to_head(v_rows).reshape(rows * row_blocks, BLK, HD)

    query_f = query_in.astype(jnp.float32)
    key_f = key_in.astype(jnp.float32)
    sums = head_sum(jnp.stack([jnp.sum(query_f * query_f, axis=1), jnp.sum(key_f * key_f, axis=1)]), "head")
    sum_query, sum_key = sums[0], sums[1]
    query_rms = lax.rsqrt(sum_query / D + EPS)
    key_rms = lax.rsqrt(sum_key / D + EPS)
    query_normed = (query_f * query_rms[:, None] * query_gain[None, :]).astype(jnp.bfloat16)
    key_normed = (key_f * key_rms[:, None] * key_gain[None, :]).astype(jnp.bfloat16)

    kq = to_head([key_normed, query_normed, out_grad])
    query_h = kq[1]
    grad_h = kq[2]

    k_all = jnp.concatenate(ring_gather(kq[0], "y", rows))

    block_ids = my_row * row_blocks + jnp.arange(row_blocks, dtype=jnp.int32)
    my_random = lax.dynamic_slice_in_dim(random_blocks.astype(jnp.int32), my_row * row_blocks, row_blocks, 0)
    glob = global_blocks.astype(jnp.int32)
    list_ids = jnp.concatenate(
        [
            block_ids[:, None] - 1,
            block_ids[:, None],
            block_ids[:, None] + 1,
            my_random,
            jnp.broadcast_to(glob[None, :], (row_blocks, GLOB)),
        ],
        axis=1,
    )
    valid = (list_ids >= 0) & (list_ids < all_blocks)
    clipped = jnp.clip(list_ids, 0, all_blocks - 1)
    shift_pos = ((my_row - clipped // row_blocks) % rows) * row_blocks + clipped % row_blocks
    target = ((clipped // row_blocks - my_row) % rows) * row_blocks + clipped % row_blocks
    out_h, dq_h, dk_own, dv_own, dk_far, dv_far = attention(
        shift_pos, target, valid.astype(jnp.int32), query_h, grad_h, k_all, v_all,
        rand_lo=3, rand_hi=3 + RAND, scale=scale,
    )

    split = lambda own, far: [own] + [far[d * row_blocks : (d + 1) * row_blocks] for d in range(rows - 1)]

    def to_tokens(arrays):
        stacked = jnp.stack([a.reshape(heads, tok_rows, HD) for a in arrays])
        moved = lax.all_to_all(stacked, "xc", 1, 1, tiled=True)
        return moved.transpose(0, 2, 1, 3).reshape(len(arrays), tok_rows, feat_dim)

    early = to_tokens([out_h, dq_h])
    own_k = ring_reduce(split(dk_own, dk_far), "y", rows)
    own_v = ring_reduce(split(dv_own, dv_far), "y", rows)

    attn_out = early[0]
    dq_normed = early[1].astype(jnp.float32)
    total_query = head_sum(jnp.sum(query_f * query_gain[None, :] * dq_normed, axis=1), "head")
    dk_normed = to_tokens([own_k.astype(jnp.bfloat16)])[0].astype(jnp.float32)
    total_key = head_sum(jnp.sum(key_f * key_gain[None, :] * dk_normed, axis=1), "head")
    value_grad = to_tokens([own_v.astype(jnp.bfloat16)])[0]
    query_grad = (
        query_rms[:, None] * query_gain[None, :] * dq_normed
        - query_f * (query_rms**3 * total_query / D)[:, None]
    ).astype(jnp.bfloat16)
    key_grad = (
        key_rms[:, None] * key_gain[None, :] * dk_normed
        - key_f * (key_rms**3 * total_key / D)[:, None]
    ).astype(jnp.bfloat16)
    return (attn_out, query_grad, key_grad, value_grad)


def solution(mesh):
    seq = mesh.shape["seq"]
    head = mesh.shape["head"]
    row = D // head // HD
    sub = Mesh(mesh.devices.reshape(seq // row, row, head), ("y", "xc", "head"))
    tok = P(("y", "xc"), "head")
    in_specs = (tok, tok, tok, tok, P("head"), P("head"), P(), P())
    out_specs = (tok, tok, tok, tok)
    return jax.shard_map(shards, mesh=sub, in_specs=in_specs, out_specs=out_specs, check_vma=False)
```

```python
import jax
import jax.numpy as jnp
import functools

from jax import lax
from jax.experimental import pallas as pl
from jax.experimental.pallas import tpu as pltpu
from jax.sharding import Mesh

from jax.sharding import PartitionSpec as P

D = 4096
HD = 128
BLK = 64
RAND = 3
GLOB = 2


EPS = 1e-06
NEG = -1e30


def attn_kernel(src_ref, tgt_ref, ok_ref, q_ref, g_ref, k_ref, v_ref,
                o_ref, dq_ref, dk_own_ref, dv_own_ref, dk_far_ref, dv_far_ref, dk_ref, dv_ref,
                *, entries, rand_lo, rand_hi, scale, group):
    step = pl.program_id(0)
    own_blocks = dk_own_ref.shape[0]

    @pl.when(step == 0)
    def _():
        dk_ref[...] = jnp.zeros_like(dk_ref)
        dv_ref[...] = jnp.zeros_like(dv_ref)

    lane_entry = lax.broadcasted_iota(jnp.int32, (1, entries * BLK), 1) // BLK
    for i in range(group):
        b = step * group + i
        q = q_ref[i]
        g = g_ref[i]
        keys = jnp.concatenate([k_ref[src_ref[b, e]] for e in range(entries)], axis=0)
        vals = jnp.concatenate([v_ref[src_ref[b, e]] for e in range(entries)], axis=0)
        ok = jnp.zeros((1, entries * BLK), jnp.int32)
        for e in range(entries):
            ok = jnp.where(lane_entry == e, ok_ref[b, e], ok)
        scores = lax.dot_general(q, keys, (((1,), (1,)), ((), ())),
                                 preferred_element_type=jnp.float32) * scale
        scores = jnp.where(ok > 0, scores, NEG)
        top = jnp.max(scores, axis=1, keepdims=True)
        expd = jnp.exp(scores - top)
        prob = expd / jnp.sum(expd, axis=1, keepdims=True)
        prob_bf = prob.astype(jnp.bfloat16)
        out = jnp.dot(prob_bf, vals, preferred_element_type=jnp.float32).astype(jnp.bfloat16)
        o_ref[i] = out
        delta = jnp.sum(g.astype(jnp.float32) * out.astype(jnp.float32), axis=1, keepdims=True)
        dprob = lax.dot_general(g, vals, (((1,), (1,)), ((), ())),
                                preferred_element_type=jnp.float32)
        dscore_bf = (prob * (dprob - delta)).astype(jnp.bfloat16)
        dq_ref[i] = (jnp.dot(dscore_bf, keys, preferred_element_type=jnp.float32) * scale).astype(jnp.bfloat16)
        dk_parts = lax.dot_general(dscore_bf, q, (((0,), (0,)), ((), ())),
                                   preferred_element_type=jnp.float32) * scale
        dv_parts = lax.dot_general(prob_bf, g, (((0,), (0,)), ((), ())),
                                   preferred_element_type=jnp.float32)
        for e in range(entries):
            pk = dk_parts[e * BLK:(e + 1) * BLK]
            pv = dv_parts[e * BLK:(e + 1) * BLK]
            if rand_lo <= e < rand_hi:
                pk = pk.astype(jnp.bfloat16).astype(jnp.float32)
                pv = pv.astype(jnp.bfloat16).astype(jnp.float32)
            t = tgt_ref[b, e]
            dk_ref[t] = dk_ref[t] + pk
            dv_ref[t] = dv_ref[t] + pv

    @pl.when(step == pl.num_programs(0) - 1)
    def _():
        dk_own_ref[...] = dk_ref[:own_blocks]
        dv_own_ref[...] = dv_ref[:own_blocks]
        dk_far_ref[...] = dk_ref[own_blocks:].astype(jnp.bfloat16)
        dv_far_ref[...] = dv_ref[own_blocks:].astype(jnp.bfloat16)


def attention(src, tgt, ok, q, g, k_all, v_all, *, rand_lo, rand_hi, scale, group=16):
    nq, entries = src.shape
    nk = k_all.shape[0]
    kern = functools.partial(attn_kernel, entries=entries, rand_lo=rand_lo, rand_hi=rand_hi,
                             scale=scale, group=group)
    blk = lambda b, *_: (b, 0, 0)
    whole = lambda b, *_: (0, 0, 0)
    grid_spec = pltpu.PrefetchScalarGridSpec(
        num_scalar_prefetch=3,
        grid=(nq // group,),
        in_specs=[
            pl.BlockSpec((group, BLK, HD), blk),
            pl.BlockSpec((group, BLK, HD), blk),
            pl.BlockSpec((nk, BLK, HD), whole),
            pl.BlockSpec((nk, BLK, HD), whole),
        ],
        out_specs=[
            pl.BlockSpec((group, BLK, HD), blk),
            pl.BlockSpec((group, BLK, HD), blk),
            pl.BlockSpec((nq, BLK, HD), whole),
            pl.BlockSpec((nq, BLK, HD), whole),
            pl.BlockSpec((nk - nq, BLK, HD), whole),
            pl.BlockSpec((nk - nq, BLK, HD), whole),
        ],
        scratch_shapes=[
            pltpu.VMEM((nk, BLK, HD), jnp.float32),
            pltpu.VMEM((nk, BLK, HD), jnp.float32),
        ],
    )
    return pl.pallas_call(
        kern,
        grid_spec=grid_spec,
        out_shape=[
            jax.ShapeDtypeStruct((nq, BLK, HD), jnp.bfloat16),
            jax.ShapeDtypeStruct((nq, BLK, HD), jnp.bfloat16),
            jax.ShapeDtypeStruct((nq, BLK, HD), jnp.float32),
            jax.ShapeDtypeStruct((nq, BLK, HD), jnp.float32),
            jax.ShapeDtypeStruct((nk - nq, BLK, HD), jnp.bfloat16),
            jax.ShapeDtypeStruct((nk - nq, BLK, HD), jnp.bfloat16),
        ],
        compiler_params=pltpu.CompilerParams(dimension_semantics=("arbitrary",), vmem_limit_bytes=48 * 1024 * 1024),
    )(src, tgt, ok, q, g, k_all, v_all)


def head_sum(value, axis):
    count = lax.axis_size(axis)
    if count & (count - 1):
        return lax.psum(value, axis)
    step = 1
    while step < count:
        value = value + lax.ppermute(value, axis, [(i, i ^ step) for i in range(count)])
        step *= 2
    return value


def ring_gather(value, axis, count):
    fwd = [(i, (i + 1) % count) for i in range(count)]
    bwd = [(i, (i - 1) % count) for i in range(count)]
    prev = lax.ppermute(value, axis, fwd)
    nxt = lax.ppermute(value, axis, bwd)
    half = value.shape[0] // 2
    far = jnp.concatenate(
        [
            lax.ppermute(prev[:half], axis, fwd),
            lax.ppermute(nxt[half:], axis, bwd),
        ]
    )
    return [value, prev, far, nxt]


def ring_reduce(pieces, axis, count):
    fwd = [(i, (i + 1) % count) for i in range(count)]
    bwd = [(i, (i - 1) % count) for i in range(count)]
    own, nxt, far, prev = pieces
    half = own.shape[0] // 2
    bf = lambda x: x.astype(jnp.bfloat16)
    f32 = lambda x: x.astype(jnp.float32)
    got_f = lax.ppermute((bf(nxt[half:]), bf(far[:half])), axis, fwd)
    got_b = lax.ppermute((bf(prev[:half]), bf(far[half:])), axis, bwd)
    late_f = lax.ppermute(bf(nxt[:half] + f32(got_f[1])), axis, fwd)
    late_b = lax.ppermute(bf(prev[half:] + f32(got_b[1])), axis, bwd)
    low = own[:half] + f32(got_b[0]) + f32(late_f)
    high = own[half:] + f32(got_f[0]) + f32(late_b)
    return jnp.concatenate([low, high])


def shards(
    query_in, key_in, value_in, out_grad, query_gain, key_gain, random_blocks, global_blocks
):
    tok_rows, feat_dim = query_in.shape
    heads = feat_dim // HD
    rows = lax.axis_size("y")
    my_row = lax.axis_index("y")
    row_tokens = tok_rows * heads
    row_blocks = row_tokens // BLK
    all_blocks = row_blocks * rows
    scale = HD ** (-0.5)

    def to_head(arrays):
        stacked = jnp.stack(arrays).reshape(len(arrays), tok_rows, heads, HD)
        stacked = stacked.transpose(0, 2, 1, 3)
        moved = lax.all_to_all(stacked, "xc", 1, 1, tiled=True)
        return moved.reshape(len(arrays), row_blocks, BLK, HD)

    v_rows = ring_gather(value_in, "y", rows)
    vg = to_head(v_rows + [out_grad])
    v_all = vg[:rows].reshape(rows * row_blocks, BLK, HD)
    grad_h = vg[rows]

    query_f = query_in.astype(jnp.float32)
    key_f = key_in.astype(jnp.float32)
    sums = head_sum(jnp.stack([jnp.sum(query_f * query_f, axis=1), jnp.sum(key_f * key_f, axis=1)]), "head")
    sum_query, sum_key = sums[0], sums[1]
    query_rms = lax.rsqrt(sum_query / D + EPS)
    key_rms = lax.rsqrt(sum_key / D + EPS)
    query_normed = (query_f * query_rms[:, None] * query_gain[None, :]).astype(jnp.bfloat16)
    key_normed = (key_f * key_rms[:, None] * key_gain[None, :]).astype(jnp.bfloat16)

    kq = to_head([key_normed, query_normed])
    query_h = kq[1]

    k_all = jnp.concatenate(ring_gather(kq[0], "y", rows))

    block_ids = my_row * row_blocks + jnp.arange(row_blocks, dtype=jnp.int32)
    my_random = lax.dynamic_slice_in_dim(random_blocks.astype(jnp.int32), my_row * row_blocks, row_blocks, 0)
    glob = global_blocks.astype(jnp.int32)
    list_ids = jnp.concatenate(
        [
            block_ids[:, None] - 1,
            block_ids[:, None],
            block_ids[:, None] + 1,
            my_random,
            jnp.broadcast_to(glob[None, :], (row_blocks, GLOB)),
        ],
        axis=1,
    )
    valid = (list_ids >= 0) & (list_ids < all_blocks)
    clipped = jnp.clip(list_ids, 0, all_blocks - 1)
    shift_pos = ((my_row - clipped // row_blocks) % rows) * row_blocks + clipped % row_blocks
    target = ((clipped // row_blocks - my_row) % rows) * row_blocks + clipped % row_blocks
    out_h, dq_h, dk_own, dv_own, dk_far, dv_far = attention(
        shift_pos, target, valid.astype(jnp.int32), query_h, grad_h, k_all, v_all,
        rand_lo=3, rand_hi=3 + RAND, scale=scale,
    )

    split = lambda own, far: [own] + [far[d * row_blocks : (d + 1) * row_blocks] for d in range(rows - 1)]

    def to_tokens(arrays):
        stacked = jnp.stack([a.reshape(heads, tok_rows, HD) for a in arrays])
        moved = lax.all_to_all(stacked, "xc", 1, 1, tiled=True)
        return moved.transpose(0, 2, 1, 3).reshape(len(arrays), tok_rows, feat_dim)

    early = to_tokens([out_h, dq_h])
    own_k = ring_reduce(split(dk_own, dk_far), "y", rows)
    own_v = ring_reduce(split(dv_own, dv_far), "y", rows)

    attn_out = early[0]
    dq_normed = early[1].astype(jnp.float32)
    total_query = head_sum(jnp.sum(query_f * query_gain[None, :] * dq_normed, axis=1), "head")
    dk_normed = to_tokens([own_k.astype(jnp.bfloat16)])[0].astype(jnp.float32)
    total_key = head_sum(jnp.sum(key_f * key_gain[None, :] * dk_normed, axis=1), "head")
    value_grad = to_tokens([own_v.astype(jnp.bfloat16)])[0]
    query_grad = (
        query_rms[:, None] * query_gain[None, :] * dq_normed
        - query_f * (query_rms**3 * total_query / D)[:, None]
    ).astype(jnp.bfloat16)
    key_grad = (
        key_rms[:, None] * key_gain[None, :] * dk_normed
        - key_f * (key_rms**3 * total_key / D)[:, None]
    ).astype(jnp.bfloat16)
    return (attn_out, query_grad, key_grad, value_grad)


def solution(mesh):
    seq = mesh.shape["seq"]
    head = mesh.shape["head"]
    row = D // head // HD
    sub = Mesh(mesh.devices.reshape(seq // row, row, head), ("y", "xc", "head"))
    tok = P(("y", "xc"), "head")
    in_specs = (tok, tok, tok, tok, P("head"), P("head"), P(), P())
    out_specs = (tok, tok, tok, tok)
    return jax.shard_map(shards, mesh=sub, in_specs=in_specs, out_specs=out_specs, check_vma=False)
```

```python
import jax
import jax.numpy as jnp
import functools

from jax import lax
from jax.experimental import pallas as pl
from jax.experimental.pallas import tpu as pltpu
from jax.sharding import Mesh

from jax.sharding import PartitionSpec as P

D = 4096
HD = 128
BLK = 64
RAND = 3
GLOB = 2


EPS = 1e-06
NEG = -1e30


def attn_kernel(src_ref, tgt_ref, ok_ref, q_ref, g_ref, k_ref, v_ref,
                o_ref, dq_ref, dk_own_ref, dv_own_ref, dk_far_ref, dv_far_ref, dk_ref, dv_ref,
                *, entries, rand_lo, rand_hi, scale, group):
    step = pl.program_id(0)
    own_blocks = dk_own_ref.shape[0]

    @pl.when(step == 0)
    def _():
        dk_ref[...] = jnp.zeros_like(dk_ref)
        dv_ref[...] = jnp.zeros_like(dv_ref)

    lane_entry = lax.broadcasted_iota(jnp.int32, (1, entries * BLK), 1) // BLK
    for i in range(group):
        b = step * group + i
        q = q_ref[i]
        g = g_ref[i]
        keys = jnp.concatenate([k_ref[src_ref[b, e]] for e in range(entries)], axis=0)
        vals = jnp.concatenate([v_ref[src_ref[b, e]] for e in range(entries)], axis=0)
        ok = jnp.zeros((1, entries * BLK), jnp.int32)
        for e in range(entries):
            ok = jnp.where(lane_entry == e, ok_ref[b, e], ok)
        scores = lax.dot_general(q, keys, (((1,), (1,)), ((), ())),
                                 preferred_element_type=jnp.float32) * scale
        scores = jnp.where(ok > 0, scores, NEG)
        top = jnp.max(scores, axis=1, keepdims=True)
        expd = jnp.exp(scores - top)
        prob = expd / jnp.sum(expd, axis=1, keepdims=True)
        prob_bf = prob.astype(jnp.bfloat16)
        out = jnp.dot(prob_bf, vals, preferred_element_type=jnp.float32).astype(jnp.bfloat16)
        o_ref[i] = out
        delta = jnp.sum(g.astype(jnp.float32) * out.astype(jnp.float32), axis=1, keepdims=True)
        dprob = lax.dot_general(g, vals, (((1,), (1,)), ((), ())),
                                preferred_element_type=jnp.float32)
        dscore_bf = (prob * (dprob - delta)).astype(jnp.bfloat16)
        dq_ref[i] = (jnp.dot(dscore_bf, keys, preferred_element_type=jnp.float32) * scale).astype(jnp.bfloat16)
        dk_parts = lax.dot_general(dscore_bf, q, (((0,), (0,)), ((), ())),
                                   preferred_element_type=jnp.float32) * scale
        dv_parts = lax.dot_general(prob_bf, g, (((0,), (0,)), ((), ())),
                                   preferred_element_type=jnp.float32)
        for e in range(entries):
            pk = dk_parts[e * BLK:(e + 1) * BLK]
            pv = dv_parts[e * BLK:(e + 1) * BLK]
            if rand_lo <= e < rand_hi:
                pk = pk.astype(jnp.bfloat16).astype(jnp.float32)
                pv = pv.astype(jnp.bfloat16).astype(jnp.float32)
            t = tgt_ref[b, e]
            dk_ref[t] = dk_ref[t] + pk
            dv_ref[t] = dv_ref[t] + pv

    @pl.when(step == pl.num_programs(0) - 1)
    def _():
        dk_own_ref[...] = dk_ref[:own_blocks]
        dv_own_ref[...] = dv_ref[:own_blocks]
        dk_far_ref[...] = dk_ref[own_blocks:].astype(jnp.bfloat16)
        dv_far_ref[...] = dv_ref[own_blocks:].astype(jnp.bfloat16)


def attention(src, tgt, ok, q, g, k_all, v_all, *, rand_lo, rand_hi, scale, group=8):
    nq, entries = src.shape
    nk = k_all.shape[0]
    kern = functools.partial(attn_kernel, entries=entries, rand_lo=rand_lo, rand_hi=rand_hi,
                             scale=scale, group=group)
    blk = lambda b, *_: (b, 0, 0)
    whole = lambda b, *_: (0, 0, 0)
    grid_spec = pltpu.PrefetchScalarGridSpec(
        num_scalar_prefetch=3,
        grid=(nq // group,),
        in_specs=[
            pl.BlockSpec((group, BLK, HD), blk),
            pl.BlockSpec((group, BLK, HD), blk),
            pl.BlockSpec((nk, BLK, HD), whole),
            pl.BlockSpec((nk, BLK, HD), whole),
        ],
        out_specs=[
            pl.BlockSpec((group, BLK, HD), blk),
            pl.BlockSpec((group, BLK, HD), blk),
            pl.BlockSpec((nq, BLK, HD), whole),
            pl.BlockSpec((nq, BLK, HD), whole),
            pl.BlockSpec((nk - nq, BLK, HD), whole),
            pl.BlockSpec((nk - nq, BLK, HD), whole),
        ],
        scratch_shapes=[
            pltpu.VMEM((nk, BLK, HD), jnp.float32),
            pltpu.VMEM((nk, BLK, HD), jnp.float32),
        ],
    )
    return pl.pallas_call(
        kern,
        grid_spec=grid_spec,
        out_shape=[
            jax.ShapeDtypeStruct((nq, BLK, HD), jnp.bfloat16),
            jax.ShapeDtypeStruct((nq, BLK, HD), jnp.bfloat16),
            jax.ShapeDtypeStruct((nq, BLK, HD), jnp.float32),
            jax.ShapeDtypeStruct((nq, BLK, HD), jnp.float32),
            jax.ShapeDtypeStruct((nk - nq, BLK, HD), jnp.bfloat16),
            jax.ShapeDtypeStruct((nk - nq, BLK, HD), jnp.bfloat16),
        ],
        compiler_params=pltpu.CompilerParams(dimension_semantics=("arbitrary",), vmem_limit_bytes=48 * 1024 * 1024),
    )(src, tgt, ok, q, g, k_all, v_all)


def head_sum(value, axis):
    count = lax.axis_size(axis)
    if count & (count - 1):
        return lax.psum(value, axis)
    me = lax.axis_index(axis)
    got = [value] + [
        lax.ppermute(value, axis, [(i, (i + d) % count) for i in range(count)])
        for d in range(1, count)
    ]
    stacked = jnp.stack(got)
    by_src = [stacked[(me - j) % count] for j in range(count)]
    while len(by_src) > 1:
        by_src = [by_src[k] + by_src[k + 1] for k in range(0, len(by_src), 2)]
    return by_src[0]


def ring_gather(value, axis, count):
    fwd = [(i, (i + 1) % count) for i in range(count)]
    bwd = [(i, (i - 1) % count) for i in range(count)]
    prev = lax.ppermute(value, axis, fwd)
    nxt = lax.ppermute(value, axis, bwd)
    half = value.shape[0] // 2
    far = jnp.concatenate(
        [
            lax.ppermute(prev[:half], axis, fwd),
            lax.ppermute(nxt[half:], axis, bwd),
        ]
    )
    return [value, prev, far, nxt]


def ring_reduce(pieces, axis, count):
    fwd = [(i, (i + 1) % count) for i in range(count)]
    bwd = [(i, (i - 1) % count) for i in range(count)]
    own, nxt, far, prev = pieces
    half = own.shape[0] // 2
    bf = lambda x: x.astype(jnp.bfloat16)
    f32 = lambda x: x.astype(jnp.float32)
    got_f = lax.ppermute((bf(nxt[half:]), bf(far[:half])), axis, fwd)
    got_b = lax.ppermute((bf(prev[:half]), bf(far[half:])), axis, bwd)
    late_f = lax.ppermute(bf(nxt[:half] + f32(got_f[1])), axis, fwd)
    late_b = lax.ppermute(bf(prev[half:] + f32(got_b[1])), axis, bwd)
    low = own[:half] + f32(got_b[0]) + f32(late_f)
    high = own[half:] + f32(got_f[0]) + f32(late_b)
    return jnp.concatenate([low, high])


def shards(
    query_in, key_in, value_in, out_grad, query_gain, key_gain, random_blocks, global_blocks
):
    tok_rows, feat_dim = query_in.shape
    heads = feat_dim // HD
    rows = lax.axis_size("y")
    my_row = lax.axis_index("y")
    row_tokens = tok_rows * heads
    row_blocks = row_tokens // BLK
    all_blocks = row_blocks * rows
    scale = HD ** (-0.5)

    def to_head(arrays):
        stacked = jnp.stack(arrays).reshape(len(arrays), tok_rows, heads, HD)
        stacked = stacked.transpose(0, 2, 1, 3)
        moved = lax.all_to_all(stacked, "xc", 1, 1, tiled=True)
        return moved.reshape(len(arrays), row_blocks, BLK, HD)

    v_rows = ring_gather(value_in, "y", rows)
    vg = to_head(v_rows + [out_grad])
    v_all = vg[:rows].reshape(rows * row_blocks, BLK, HD)
    grad_h = vg[rows]

    query_f = query_in.astype(jnp.float32)
    key_f = key_in.astype(jnp.float32)
    sums = head_sum(jnp.stack([jnp.sum(query_f * query_f, axis=1), jnp.sum(key_f * key_f, axis=1)]), "head")
    sum_query, sum_key = sums[0], sums[1]
    query_rms = lax.rsqrt(sum_query / D + EPS)
    key_rms = lax.rsqrt(sum_key / D + EPS)
    query_normed = (query_f * query_rms[:, None] * query_gain[None, :]).astype(jnp.bfloat16)
    key_normed = (key_f * key_rms[:, None] * key_gain[None, :]).astype(jnp.bfloat16)

    kq = to_head([key_normed, query_normed])
    query_h = kq[1]

    k_all = jnp.concatenate(ring_gather(kq[0], "y", rows))

    block_ids = my_row * row_blocks + jnp.arange(row_blocks, dtype=jnp.int32)
    my_random = lax.dynamic_slice_in_dim(random_blocks.astype(jnp.int32), my_row * row_blocks, row_blocks, 0)
    glob = global_blocks.astype(jnp.int32)
    list_ids = jnp.concatenate(
        [
            block_ids[:, None] - 1,
            block_ids[:, None],
            block_ids[:, None] + 1,
            my_random,
            jnp.broadcast_to(glob[None, :], (row_blocks, GLOB)),
        ],
        axis=1,
    )
    valid = (list_ids >= 0) & (list_ids < all_blocks)
    clipped = jnp.clip(list_ids, 0, all_blocks - 1)
    shift_pos = ((my_row - clipped // row_blocks) % rows) * row_blocks + clipped % row_blocks
    target = ((clipped // row_blocks - my_row) % rows) * row_blocks + clipped % row_blocks
    out_h, dq_h, dk_own, dv_own, dk_far, dv_far = attention(
        shift_pos, target, valid.astype(jnp.int32), query_h, grad_h, k_all, v_all,
        rand_lo=3, rand_hi=3 + RAND, scale=scale,
    )

    split = lambda own, far: [own] + [far[d * row_blocks : (d + 1) * row_blocks] for d in range(rows - 1)]

    def to_tokens(arrays):
        stacked = jnp.stack([a.reshape(heads, tok_rows, HD) for a in arrays])
        moved = lax.all_to_all(stacked, "xc", 1, 1, tiled=True)
        return moved.transpose(0, 2, 1, 3).reshape(len(arrays), tok_rows, feat_dim)

    early = to_tokens([out_h, dq_h])
    own_k = ring_reduce(split(dk_own, dk_far), "y", rows)
    own_v = ring_reduce(split(dv_own, dv_far), "y", rows)

    attn_out = early[0]
    dq_normed = early[1].astype(jnp.float32)
    total_query = head_sum(jnp.sum(query_f * query_gain[None, :] * dq_normed, axis=1), "head")
    dk_normed = to_tokens([own_k.astype(jnp.bfloat16)])[0].astype(jnp.float32)
    total_key = head_sum(jnp.sum(key_f * key_gain[None, :] * dk_normed, axis=1), "head")
    value_grad = to_tokens([own_v.astype(jnp.bfloat16)])[0]
    query_grad = (
        query_rms[:, None] * query_gain[None, :] * dq_normed
        - query_f * (query_rms**3 * total_query / D)[:, None]
    ).astype(jnp.bfloat16)
    key_grad = (
        key_rms[:, None] * key_gain[None, :] * dk_normed
        - key_f * (key_rms**3 * total_key / D)[:, None]
    ).astype(jnp.bfloat16)
    return (attn_out, query_grad, key_grad, value_grad)


def solution(mesh):
    seq = mesh.shape["seq"]
    head = mesh.shape["head"]
    row = D // head // HD
    sub = Mesh(mesh.devices.reshape(seq // row, row, head), ("y", "xc", "head"))
    tok = P(("y", "xc"), "head")
    in_specs = (tok, tok, tok, tok, P("head"), P("head"), P(), P())
    out_specs = (tok, tok, tok, tok)
    return jax.shard_map(shards, mesh=sub, in_specs=in_specs, out_specs=out_specs, check_vma=False)
```
